512 devices in a mesh: grp: 16 (over z, core), dev: 32 (over x, y).
Axes of the slice: x: 4, y: 8, z: 8, core: 2. Of those that a mesh axis runs over, the one named last changes fastest.
Arguments:
- ssm_input: bfloat16 [4096, 4096], P('grp', 'dev'), may hold values from -6 to 6
- gate_input: bfloat16 [4096, 4096], P('grp', 'dev'), may hold values from -6 to 6
- step_size: float32 [4096, 64], P('grp', 'dev'), may hold values from 6.1035156e-05 to 0.3375
- decay_rate: float32 [64], P('dev'), may hold values from 0.5 to 2
- in_coeff: bfloat16 [4096, 128], P('grp'), may hold values from -6 to 6
- out_coeff: bfloat16 [4096, 128], P('grp'), may hold values from -6 to 6
- skip_gain: float32 [64], P('dev'), may hold values from 0.5 to 3
- norm_gain: float32 [4096], P('dev'), may hold values from 0.5 to 1.5
- out_proj: bfloat16 [4096, 2048], P(None, 'dev'), may hold values from -0.09375 to 0.09375
- residual: bfloat16 [4096, 2048], P(('grp', 'dev')), may hold values from -6 to 6
- ffn_gain: float32 [2048], replicated, may hold values from 0.5 to 1.5
- router: float32 [2048, 16], replicated, may hold values from -0.125 to 0.125
- routes: int32 [4096, 2], P(('grp', 'dev')), may hold values from 0 to 15, all different within a row; in each aligned block of 8 rows (0 to 7, 8 to 15, ...) at most 2 rows name the same one
- gate_weight: bfloat16 [16, 2048, 8192], P('grp', None, 'dev'), may hold values from -0.125 to 0.125
- up_weight: bfloat16 [16, 2048, 8192], P('grp', None, 'dev'), may hold values from -0.125 to 0.125
- down_weight: bfloat16 [16, 8192, 2048], P('grp', 'dev'), may hold values from -0.0625 to 0.0625
Outputs:
- moe_out: bfloat16 [4096, 2048], P(('grp', 'dev'))
The draws below stay inside these ranges and needn't reach their ends.
Inputs may be any that keep to these rules, and one draw needn't show every extreme that they name: `routes`: each row names two different experts; among the 8 rows of one dispatch block of consecutive tokens no expert is named more than 2 times, a bound that some block reaches.
All inputs are finite; a program needn't handle non-finite values.
Results may differ from the reference program's by a relative error of at most 0.012.
Values may be sent and summed in bfloat16 or wider, within the bound.
No kernel may reach another device: no remote copies, remote signals or barrier semaphores. Data moves between devices by JAX's collectives and lax.ppermute only.
A program may use at most 64 MiB of HBM per device.

```python
import math
import jax
import jax.numpy as jnp
import numpy as np
from jax import lax

MODEL_DIM = 2048
NUM_HEADS = 64
HEAD_DIM = 64
STATE_DIM = 128
HIDDEN_DIM = 8192
EXPERTS = 16
STRING_LENGTH = 4096
TOK_DEV = 8
INNER_DIM = 4096
HID_DEV = 256
SLOT_CAP = 2


def draw_step_size(key, part):
    gradual_seed, jagged_seed, spike_seed = jax.random.split(key, 3)
    slow_share = 0.5
    slow_heads = jax.random.bernoulli(gradual_seed, slow_share, (NUM_HEADS,))
    jaggedness = jax.random.uniform(jagged_seed, (STRING_LENGTH, NUM_HEADS), jnp.float32, 0.5, 1.5)
    baseline_frequency = jnp.where(slow_heads, 0.5 / STRING_LENGTH, 1.0 / 40.0)
    spike_indices = jax.random.randint(spike_seed, (4,), 0, STRING_LENGTH)
    element_ordinals = jnp.arange(STRING_LENGTH)
    spike_present = jnp.any(element_ordinals[:, None] == spike_indices[None, :], axis=1)
    return (baseline_frequency[None, :] * jaggedness + jnp.where(spike_present, 0.3, 0.0)[:, None]).astype(jnp.float32)


def block_levels(own_key, dims, cuts, least, top_value):
    factor_of, own = 1.0, jax.random.fold_in(own_key, 6)
    for position, shards_of in cuts:
        draws = jnp.exp(jax.random.uniform(jax.random.fold_in(own, position), (shards_of,), jnp.float32, least / len(cuts), top_value / len(cuts)))
        factor_of = factor_of * jnp.repeat(draws, dims[position] // shards_of).reshape([-1 if axis == position else 1 for axis in range(len(dims))])
    return factor_of


def routed_block(rng, own, number, rows, amount, top, reach, slope):
    order = jax.random.permutation(rng, amount)
    heavy_load, common = shares(amount, rows * top, reach, slope, True), shares(amount, rows * top, reach, slope, False)
    places = jnp.arange(amount)

    def named(sizes, offset_by):
        used = int((sizes > 0).sum())
        fixed = max(1, used // 4)
        shifted = fixed + (places - fixed + offset_by * (used - fixed)) % max(1, amount - fixed)
        return jnp.zeros((amount,), jnp.int32).at[order[jnp.where(places < fixed, places, shifted)]].set(jnp.asarray(sizes, jnp.int32))

    sizes = jnp.where(number % 4 == 0, named(heavy_load, number // 4), named(common, number - number // 4 - 1))
    mixed = jax.random.permutation(jax.random.fold_in(own, 3), amount)
    donor, sink = mixed[0:amount // 2 * 2:2], mixed[1:amount // 2 * 2:2]
    slack = jnp.minimum(sizes[donor] - 1, reach - sizes[sink]) // 2
    slack = jnp.where((donor == order[0]) | (sink == order[0]) | (sizes[sink] == 0), 0, jnp.maximum(slack, 0))
    shifted = jax.random.randint(jax.random.fold_in(own, 4), (amount // 2,), 0, 1 << 20) % (slack + 1)
    sizes = sizes.at[donor].add(-shifted).at[sink].add(shifted)
    items = jnp.searchsorted(jnp.cumsum(sizes), jnp.arange(rows * top), side="right").astype(jnp.int32)
    table = items.reshape(top, rows).T
    table = table[jax.random.permutation(jax.random.fold_in(own, 1), rows)]
    offset_by = jax.random.randint(jax.random.fold_in(own, 2), (rows, 1), 0, top)
    return jnp.take_along_axis(table, (jnp.arange(top)[None, :] + offset_by) % top, axis=1)


def shares(amount, total, limit, slope, full):
    loads = [(1 << 20) // math.isqrt(standing ** slope) + 1 for standing in range(1, amount + 1)]
    largest = limit if full else min(limit, max(-(-total // amount), total * loads[0] // sum(loads)))
    least = 1 if total - largest >= amount - 1 else 0
    holding, spare = [largest] + [least] * (amount - 1), total - largest - least * (amount - 1)
    while spare > 0:
        candidates = [i for i in range(1, amount) if holding[i] < largest] or [i for i in range(1, amount) if holding[i] < limit]
        mass, remaining = sum([loads[i] for i in candidates]), spare
        for i in candidates:
            more = min(limit - holding[i], max(1, remaining * loads[i] // mass), spare)
            holding[i] = holding[i] + more
            spare = spare - more
    return np.array(holding)


def centred(rng, shape, width, limit, shards=(), kind=jnp.bfloat16):
    result = jax.random.normal(rng, shape, jnp.float32) * width
    if len(shards) > 0:
        result = block_levels(rng, shape, shards, -0.22, 0.18) * result
    return jnp.clip(result, min=-limit, max=limit).astype(kind)


def setup_inputs(seed: int = 0) -> dict:
    key_of = jax.random.split(jax.random.key(seed), 17)
    ssm_input = centred(key_of[0], (STRING_LENGTH, INNER_DIM), 1.0, 6.0, ((0, 16), (1, 32)))
    gate_input = centred(key_of[1], (STRING_LENGTH, INNER_DIM), 1.0, 6.0, ((0, 16), (1, 32)))
    step_size = draw_step_size(jax.random.fold_in(key_of[16], 71), 0)
    decay_rate = jnp.clip(jnp.exp(math.log(2.0) - 1.3862944 * jax.random.uniform(key_of[3], (NUM_HEADS,), jnp.float32) ** block_levels(key_of[3], (NUM_HEADS,), ((0, 32),), -0.2, 0.2)), 0.5, 2.0)
    in_coeff = centred(key_of[4], (STRING_LENGTH, STATE_DIM), 1.0, 6.0, ((0, 16),))
    out_coeff = centred(key_of[5], (STRING_LENGTH, STATE_DIM), 1.0, 6.0, ((0, 16),))
    skip_gain = jnp.clip(jnp.exp(math.log(3.0) - 1.7917595 * jax.random.uniform(key_of[6], (NUM_HEADS,), jnp.float32) ** block_levels(key_of[6], (NUM_HEADS,), ((0, 32),), -0.2, 0.2)), 0.5, 3.0)
    norm_gain = jnp.clip(1.0 + 0.1 * jax.random.normal(key_of[7], (INNER_DIM,), jnp.float32), 0.5, 1.5)
    out_proj = centred(key_of[8], (INNER_DIM, MODEL_DIM), INNER_DIM ** -0.5, 0.09375, ((1, 32),))
    residual = centred(key_of[9], (STRING_LENGTH, MODEL_DIM), 1.0, 6.0, ((0, 512),))
    ffn_gain = jnp.clip(1.0 + 0.1 * jax.random.normal(key_of[10], (MODEL_DIM,), jnp.float32), 0.5, 1.5)
    router = centred(key_of[11], (MODEL_DIM, EXPERTS), MODEL_DIM ** -0.5, 0.125, (), jnp.float32)
    routes_keys = jax.random.split(jax.random.fold_in(key_of[12], 1), STRING_LENGTH // TOK_DEV)
    routes_turns = jax.random.permutation(jax.random.fold_in(key_of[12], 3), STRING_LENGTH // TOK_DEV)
    routes = jax.vmap(lambda own, number: routed_block(jax.random.fold_in(key_of[12], 2), own, number, TOK_DEV, EXPERTS, 2, SLOT_CAP, 2))(routes_keys, routes_turns).reshape((STRING_LENGTH, 2))
    gate_weight = centred(key_of[13], (EXPERTS, MODEL_DIM, HIDDEN_DIM), MODEL_DIM ** -0.5, 0.125, ((0, 16), (2, 32)))
    up_weight = centred(key_of[14], (EXPERTS, MODEL_DIM, HIDDEN_DIM), MODEL_DIM ** -0.5, 0.125, ((0, 16), (2, 32)))
    down_weight = centred(key_of[15], (EXPERTS, HIDDEN_DIM, MODEL_DIM), HIDDEN_DIM ** -0.5, 0.0625, ((0, 16), (1, 32)))
    return dict(ssm_input=ssm_input, gate_input=gate_input, step_size=step_size, decay_rate=decay_rate, in_coeff=in_coeff, out_coeff=out_coeff, skip_gain=skip_gain, norm_gain=norm_gain, out_proj=out_proj, residual=residual, ffn_gain=ffn_gain, router=router, routes=routes, gate_weight=gate_weight, up_weight=up_weight, down_weight=down_weight)


EPSILON = 1e-05
HIGHEST_PREC = lax.Precision.HIGHEST

def rms_scale(values, gain_vec):
    return values * lax.rsqrt(lax.optimization_barrier(jnp.mean(values * values, axis=-1, keepdims=True)) + EPSILON) * gain_vec

def slot_tables(routes_block, expert_count, slot_cap):
    blocks, row_total = (routes_block.shape[0], routes_block.shape[1])
    flat_routes = routes_block.reshape(blocks, row_total * 2)
    onehot = (flat_routes[:, :, None] == jnp.arange(expert_count, dtype=jnp.int32)[None, None, :]).astype(jnp.int32)
    earlier = jnp.cumsum(onehot, axis=1) - onehot
    slot_rank = lax.optimization_barrier(jnp.sum(earlier * onehot, axis=2))
    slot_index = (flat_routes * slot_cap + slot_rank).reshape(blocks, row_total, 2)
    placed = slot_index[:, :, :, None] == jnp.arange(expert_count * slot_cap, dtype=jnp.int32)[None, None, None, :]
    return placed.astype(jnp.float32)

def reference(ssm_input, gate_input, step_size, decay_rate, in_coeff, out_coeff, skip_gain, norm_gain, out_proj, residual, ffn_gain, router, routes, gate_weight, up_weight, down_weight):
    inputs_f = ssm_input.astype(jnp.float32).reshape(STRING_LENGTH, NUM_HEADS, HEAD_DIM)
    in_float = in_coeff.astype(jnp.float32)
    out_float = out_coeff.astype(jnp.float32)

    def advance(ssm_state, token_row):
        x_row, step_row, in_row, out_row = token_row
        factor = jnp.exp(-step_row * decay_rate)
        ssm_state = factor[:, None, None] * ssm_state + (step_row[:, None] * x_row)[:, :, None] * in_row[None, None, :]
        output = jnp.einsum('hpn,n->hp', ssm_state, out_row, precision=HIGHEST_PREC)
        return (ssm_state, output)
    initial = jnp.zeros((NUM_HEADS, HEAD_DIM, STATE_DIM), jnp.float32)
    final_state, scanned = lax.scan(advance, initial, (inputs_f, step_size, in_float, out_float))
    ssm_out = scanned + skip_gain[None, :, None] * inputs_f
    gated_out = ssm_out.reshape(STRING_LENGTH, INNER_DIM) * jax.nn.silu(gate_input.astype(jnp.float32))
    mixed_rows = rms_scale(gated_out, norm_gain).astype(jnp.bfloat16)
    mamba_out = jnp.dot(mixed_rows, out_proj, preferred_element_type=jnp.float32).astype(jnp.bfloat16)
    hidden_res = (residual.astype(jnp.float32) + mamba_out.astype(jnp.float32)).astype(jnp.bfloat16)
    hidden_float = hidden_res.astype(jnp.float32)
    normed = rms_scale(hidden_float, ffn_gain).astype(jnp.bfloat16)
    logits = jnp.dot(normed.astype(jnp.float32), router, precision=HIGHEST_PREC)
    expert_ids = jnp.arange(EXPERTS, dtype=jnp.int32)[None, :]
    first_logit = lax.optimization_barrier(jnp.sum(logits * (routes[:, 0:1] == expert_ids).astype(jnp.float32), axis=1))
    second_logit = lax.optimization_barrier(jnp.sum(logits * (routes[:, 1:2] == expert_ids).astype(jnp.float32), axis=1))
    first_prob = jax.nn.sigmoid(first_logit - second_logit)
    second_prob = 1.0 - first_prob
    blocks = STRING_LENGTH // TOK_DEV
    placed = slot_tables(routes.reshape(blocks, TOK_DEV, 2), EXPERTS, SLOT_CAP)
    filled = lax.optimization_barrier(jnp.sum(placed, axis=2))
    normed_blocks = normed.astype(jnp.float32).reshape(blocks, TOK_DEV, MODEL_DIM)
    dispatch = jnp.einsum('brs,brm->bsm', filled, normed_blocks, precision=HIGHEST_PREC).astype(jnp.bfloat16)
    dispatch = dispatch.reshape(blocks, EXPERTS, SLOT_CAP, MODEL_DIM).transpose(1, 0, 2, 3)
    block_count = HIDDEN_DIM // HID_DEV

    def run_expert(operands):
        expert_rows, gate_w, up_w, down_w = operands
        flat_rows = expert_rows.reshape(blocks * SLOT_CAP, MODEL_DIM)
        gate_act = jnp.dot(flat_rows, gate_w, preferred_element_type=jnp.float32)
        up_act = jnp.dot(flat_rows, up_w, preferred_element_type=jnp.float32)
        hidden = (jax.nn.silu(gate_act) * up_act).astype(jnp.bfloat16)
        hidden_blocks = hidden.reshape(blocks * SLOT_CAP, block_count, HID_DEV).transpose(1, 0, 2)
        down_blocks = down_w.reshape(block_count, HID_DEV, MODEL_DIM)

        def add_block(running, pair_in):
            partial_sum = jnp.dot(pair_in[0], pair_in[1], preferred_element_type=jnp.float32).astype(jnp.bfloat16)
            partial_sum = lax.optimization_barrier(partial_sum)
            return (running + partial_sum.astype(jnp.float32), None)
        summed, unused = lax.scan(add_block, jnp.zeros((blocks * SLOT_CAP, MODEL_DIM), jnp.float32), (hidden_blocks, down_blocks))
        return summed.astype(jnp.bfloat16).reshape(blocks, SLOT_CAP, MODEL_DIM)
    expert_out = lax.map(run_expert, (dispatch, gate_weight, up_weight, down_weight))
    returned = expert_out.transpose(1, 0, 2, 3).reshape(blocks, EXPERTS * SLOT_CAP, MODEL_DIM).astype(jnp.float32)
    first_blocks = first_prob.reshape(blocks, TOK_DEV)
    second_blocks = second_prob.reshape(blocks, TOK_DEV)
    weights = first_blocks[:, :, None] * placed[:, :, 0, :] + second_blocks[:, :, None] * placed[:, :, 1, :]
    contrib = jnp.einsum('brs,bsm->brm', weights, returned, precision=HIGHEST_PREC).reshape(STRING_LENGTH, MODEL_DIM)
    return (hidden_float + contrib).astype(jnp.bfloat16)
```

```python
import jax
import jax.numpy as jnp
from jax import lax
from jax.sharding import Mesh
from jax.sharding import PartitionSpec as P

DEV = ("dev_0", "dev_1")
GRP_DEV = ("grp", "dev_0", "dev_1")


EPSILON = 1e-05
HIGHEST_PREC = lax.Precision.HIGHEST


def side_by_side(arrays, axis, dim, along):
    columns = [a.reshape(*a.shape[:along], -1) for a in arrays]
    both = jnp.concatenate(columns, axis=along)
    filled, at, finished = (lax.all_gather(both, axis, axis=dim, tiled=True), 0, [])
    for a, column in zip(arrays, columns):
        piece = filled[..., at : at + column.shape[along]]
        finished.append(piece.reshape(*piece.shape[:along], *a.shape[along:]))
        at += column.shape[along]
    return tuple(finished)


def sent_to_all(shard, axis):
    peers = lax.axis_size(axis)
    return lax.all_to_all(
        jnp.broadcast_to(shard[None], (peers, *shard.shape)), axis, 0, 0, tiled=True
    )


def of_everyone(shard, axis):
    everything = sent_to_all(shard, axis)
    return jnp.sum(everything, axis=0)


def in_order(tiles, dim):
    dims = list(tiles.shape[1:])
    dims[dim] *= tiles.shape[0]
    return jnp.moveaxis(tiles, 0, dim).reshape(dims)


def collect(shard, axis, dim):
    return in_order(sent_to_all(shard, axis), dim)


def sum_by_axis(terms, axes):
    total = terms.astype(jnp.bfloat16)
    total = lax.psum_scatter(total, axes, scatter_dimension=0, tiled=True)
    return total.astype(jnp.float32)


def rms_scale(values, gain_vec):
    return (
        values * lax.rsqrt(jnp.mean(values * values, axis=-1, keepdims=True) + EPSILON) * gain_vec
    )


def slot_tables(routes_block, expert_count, slot_cap):
    blocks, row_total = (routes_block.shape[0], routes_block.shape[1])
    flat_routes = routes_block.reshape(blocks, row_total * 2)
    onehot = (
        flat_routes[:, :, None] == jnp.arange(expert_count, dtype=jnp.int32)[None, None, :]
    ).astype(jnp.int32)
    earlier = jnp.cumsum(onehot, axis=1) - onehot
    slot_rank = jnp.sum(earlier * onehot, axis=2)
    slot_index = (flat_routes * slot_cap + slot_rank).reshape(blocks, row_total, 2)
    placed = (
        slot_index[:, :, :, None]
        == jnp.arange(expert_count * slot_cap, dtype=jnp.int32)[None, None, None, :]
    )
    return placed.astype(jnp.float32)


def shards(
    ssm_input,
    gate_input,
    step_size,
    decay_rate,
    in_coeff,
    out_coeff,
    skip_gain,
    norm_gain,
    out_proj,
    residual,
    ffn_gain,
    router,
    routes,
    gate_weight,
    up_weight,
    down_weight,
):
    tok_rows = ssm_input.shape[0]
    head_count = step_size.shape[1]
    head_width = ssm_input.shape[1] // head_count
    dev_count = lax.axis_size(DEV)
    inner_dim = ssm_input.shape[1] * dev_count
    block_rows = residual.shape[0]
    model_dim = residual.shape[1]
    experts = lax.axis_size("grp")
    slot_cap = max(2, 4 * block_rows // experts)
    group_slots = experts * slot_cap
    inputs_f = ssm_input.astype(jnp.float32).reshape(tok_rows, head_count, head_width)
    in_float = in_coeff.astype(jnp.float32)
    out_float = out_coeff.astype(jnp.float32)
    log_rate = -(step_size * decay_rate[None, :])
    cumulative = jnp.cumsum(log_rate, axis=0)
    causal = (jnp.arange(tok_rows)[:, None] >= jnp.arange(tok_rows)[None, :])[:, :, None]
    spread = cumulative[:, None, :] - cumulative[None, :, :]
    decay_pair = jnp.where(causal, jnp.exp(jnp.where(causal, spread, 0.0)), 0.0)
    scores = jnp.dot(out_coeff, in_coeff.T, preferred_element_type=jnp.float32)
    mixing = decay_pair * scores[:, :, None] * step_size[None, :, :]
    inside = jnp.einsum("tuh,uhp->thp", mixing, inputs_f, precision=HIGHEST_PREC)
    to_end = jnp.exp(cumulative[-1][None, :] - cumulative) * step_size
    own_state = jnp.einsum("uh,uhp,un->hpn", to_end, inputs_f, in_float, precision=HIGHEST_PREC)
    own_log = cumulative[-1]
    group_logs, group_states = tuple(
        (
            part.astype(jnp.float32)
            for part in side_by_side(
                (own_log[None].astype(jnp.bfloat16), own_state[None].astype(jnp.bfloat16)),
                "grp",
                0,
                2,
            )
        )
    )
    group_index = jnp.arange(group_logs.shape[0])
    my_group = lax.axis_index("grp")
    inclusive = jnp.cumsum(group_logs, axis=0)
    exclusive = inclusive - group_logs
    before_me = jnp.sum(jnp.where((group_index == my_group)[:, None], exclusive, 0.0), axis=0)
    earlier_mask = (group_index < my_group)[:, None]
    weighting = jnp.where(
        earlier_mask, jnp.exp(jnp.where(earlier_mask, before_me[None, :] - inclusive, 0.0)), 0.0
    )
    entering = jnp.einsum("gh,ghpn->hpn", weighting, group_states, precision=HIGHEST_PREC)
    carried = jnp.exp(cumulative)[:, :, None] * jnp.einsum(
        "hpn,tn->thp", entering, out_float, precision=HIGHEST_PREC
    )
    ssm_out = inside + carried + skip_gain[None, :, None] * inputs_f
    gated_out = ssm_out.reshape(tok_rows, head_count * head_width) * jax.nn.silu(
        gate_input.astype(jnp.float32)
    )
    squares = lax.psum(jnp.sum(gated_out * gated_out, axis=1), DEV)
    mixed_rows = (
        gated_out * lax.rsqrt(squares[:, None] / inner_dim + EPSILON) * norm_gain[None, :]
    ).astype(jnp.bfloat16)
    gathered = lax.all_gather(mixed_rows, DEV, axis=0)
    projected = jnp.einsum(
        "dtc,dcf->tf",
        gathered,
        out_proj.reshape(dev_count, -1, out_proj.shape[1]),
        preferred_element_type=jnp.float32,
    ).astype(jnp.bfloat16)
    mamba_out = lax.all_to_all(projected, DEV, split_axis=0, concat_axis=1, tiled=True)
    hidden_res = (residual.astype(jnp.float32) + mamba_out.astype(jnp.float32)).astype(jnp.bfloat16)
    hidden_float = hidden_res.astype(jnp.float32)
    normed = rms_scale(hidden_float, ffn_gain).astype(jnp.bfloat16)
    logits = jnp.dot(normed.astype(jnp.float32), router, precision=HIGHEST_PREC)
    expert_ids = jnp.arange(experts, dtype=jnp.int32)[None, :]
    first_logit = jnp.sum(logits * (routes[:, 0:1] == expert_ids).astype(jnp.float32), axis=1)
    second_logit = jnp.sum(logits * (routes[:, 1:2] == expert_ids).astype(jnp.float32), axis=1)
    first_prob = jax.nn.sigmoid(first_logit - second_logit)
    second_prob = 1.0 - first_prob
    placed = slot_tables(routes[None], experts, slot_cap)[0]
    filled = jnp.sum(placed, axis=1)
    outgoing = jnp.dot(
        filled.T.astype(jnp.bfloat16), normed, preferred_element_type=jnp.float32
    ).astype(jnp.bfloat16)
    outgoing = outgoing.reshape(experts, slot_cap, model_dim)
    arrived = lax.all_to_all(outgoing, "grp", split_axis=0, concat_axis=0, tiled=True)
    all_rows = lax.all_gather(arrived, DEV, axis=0, tiled=True).reshape(-1, model_dim)
    gate_act = jnp.dot(all_rows, gate_weight[0], preferred_element_type=jnp.float32)
    up_act = jnp.dot(all_rows, up_weight[0], preferred_element_type=jnp.float32)
    hidden = (jax.nn.silu(gate_act) * up_act).astype(jnp.bfloat16)
    summed = sum_by_axis(jnp.dot(hidden, down_weight[0], preferred_element_type=jnp.float32), DEV)
    returned = lax.all_to_all(
        summed.astype(jnp.bfloat16).reshape(experts, slot_cap, model_dim),
        "grp",
        split_axis=0,
        concat_axis=0,
        tiled=True,
    )
    weights = first_prob[:, None] * placed[:, 0, :] + second_prob[:, None] * placed[:, 1, :]
    contrib = jnp.dot(
        weights,
        returned.reshape(group_slots, model_dim).astype(jnp.float32),
        precision=HIGHEST_PREC,
    )
    return (hidden_float + contrib).astype(jnp.bfloat16)


def solution(mesh):
    torus = Mesh(mesh.devices.reshape(mesh.shape["grp"], 4, 8), ("grp", "dev_0", "dev_1"))
    in_specs = (
        P("grp", DEV),
        P("grp", DEV),
        P("grp", DEV),
        P(DEV),
        P("grp", None),
        P("grp", None),
        P(DEV),
        P(DEV),
        P(None, DEV),
        P(GRP_DEV, None),
        P(),
        P(),
        P(GRP_DEV, None),
        P("grp", None, DEV),
        P("grp", None, DEV),
        P("grp", DEV, None),
    )
    out_specs = P(GRP_DEV, None)
    return jax.shard_map(
        shards, mesh=torus, in_specs=in_specs, out_specs=out_specs, check_vma=False
    )
```

```python
import jax
import jax.numpy as jnp
from jax import lax
from jax.sharding import Mesh
from jax.sharding import PartitionSpec as P

DEV = ("dev_0", "dev_1")
GRP_DEV = ("grp", "dev_0", "dev_1")


EPSILON = 1e-05
HIGHEST_PREC = lax.Precision.HIGHEST


def side_by_side(arrays, axis, dim, along):
    columns = [a.reshape(*a.shape[:along], -1) for a in arrays]
    both = jnp.concatenate(columns, axis=along)
    filled, at, finished = (lax.all_gather(both, axis, axis=dim, tiled=True), 0, [])
    for a, column in zip(arrays, columns):
        piece = filled[..., at : at + column.shape[along]]
        finished.append(piece.reshape(*piece.shape[:along], *a.shape[along:]))
        at += column.shape[along]
    return tuple(finished)


def sent_to_all(shard, axis):
    peers = lax.axis_size(axis)
    return lax.all_to_all(
        jnp.broadcast_to(shard[None], (peers, *shard.shape)), axis, 0, 0, tiled=True
    )


def of_everyone(shard, axis):
    everything = sent_to_all(shard, axis)
    return jnp.sum(everything, axis=0)


def in_order(tiles, dim):
    dims = list(tiles.shape[1:])
    dims[dim] *= tiles.shape[0]
    return jnp.moveaxis(tiles, 0, dim).reshape(dims)


def collect(shard, axis, dim):
    return in_order(sent_to_all(shard, axis), dim)


def sum_by_axis(terms, axes):
    total = terms.astype(jnp.bfloat16)
    for axis in axes:
        total = lax.psum_scatter(total, axis, scatter_dimension=0, tiled=True)
    return total.astype(jnp.float32)


def ring_gather(shard, axis):
    size = lax.axis_size(axis)
    forward, backward, pieces = shard, shard, {0: shard}
    for step in range(1, size // 2 + 1):
        forward = lax.ppermute(forward, axis, [(i, (i + 1) % size) for i in range(size)])
        pieces[-step] = forward
        if step < size - step:
            backward = lax.ppermute(backward, axis, [(i, (i - 1) % size) for i in range(size)])
            pieces[step] = backward
    offsets = list(range(-(size // 2), size - size // 2))
    stacked = jnp.stack([pieces[o] for o in offsets])
    doubled = jnp.concatenate([stacked, stacked])
    start = (-offsets[0] - lax.axis_index(axis)) % size
    return lax.dynamic_slice_in_dim(doubled, start, size, 0)


def rms_scale(values, gain_vec):
    return (
        values * lax.rsqrt(jnp.mean(values * values, axis=-1, keepdims=True) + EPSILON) * gain_vec
    )


def slot_tables(routes_block, expert_count, slot_cap):
    blocks, row_total = (routes_block.shape[0], routes_block.shape[1])
    flat_routes = routes_block.reshape(blocks, row_total * 2)
    onehot = (
        flat_routes[:, :, None] == jnp.arange(expert_count, dtype=jnp.int32)[None, None, :]
    ).astype(jnp.int32)
    earlier = jnp.cumsum(onehot, axis=1) - onehot
    slot_rank = jnp.sum(earlier * onehot, axis=2)
    slot_index = (flat_routes * slot_cap + slot_rank).reshape(blocks, row_total, 2)
    placed = (
        slot_index[:, :, :, None]
        == jnp.arange(expert_count * slot_cap, dtype=jnp.int32)[None, None, None, :]
    )
    return placed.astype(jnp.float32)


def shards(
    ssm_input,
    gate_input,
    step_size,
    decay_rate,
    in_coeff,
    out_coeff,
    skip_gain,
    norm_gain,
    out_proj,
    residual,
    ffn_gain,
    router,
    routes,
    gate_weight,
    up_weight,
    down_weight,
):
    tok_rows = ssm_input.shape[0]
    head_count = step_size.shape[1]
    head_width = ssm_input.shape[1] // head_count
    dev_count = lax.axis_size(DEV)
    inner_dim = ssm_input.shape[1] * dev_count
    block_rows = residual.shape[0]
    model_dim = residual.shape[1]
    experts = lax.axis_size("grp")
    slot_cap = max(2, 4 * block_rows // experts)
    group_slots = experts * slot_cap
    inputs_f = ssm_input.astype(jnp.float32).reshape(tok_rows, head_count, head_width)
    in_float = in_coeff.astype(jnp.float32)
    out_float = out_coeff.astype(jnp.float32)
    log_rate = -(step_size * decay_rate[None, :])
    cumulative = jnp.cumsum(log_rate, axis=0)
    causal = (jnp.arange(tok_rows)[:, None] >= jnp.arange(tok_rows)[None, :])[:, :, None]
    spread = cumulative[:, None, :] - cumulative[None, :, :]
    decay_pair = jnp.where(causal, jnp.exp(jnp.where(causal, spread, 0.0)), 0.0)
    scores = jnp.dot(out_coeff, in_coeff.T, preferred_element_type=jnp.float32)
    mixing = decay_pair * scores[:, :, None] * step_size[None, :, :]
    inside = jnp.einsum("tuh,uhp->thp", mixing, inputs_f, precision=HIGHEST_PREC)
    to_end = jnp.exp(cumulative[-1][None, :] - cumulative) * step_size
    own_state = jnp.einsum("uh,uhp,un->hpn", to_end, inputs_f, in_float, precision=HIGHEST_PREC)
    own_log = cumulative[-1]
    group_logs, group_states = tuple(
        (
            part.astype(jnp.float32)
            for part in side_by_side(
                (own_log[None].astype(jnp.bfloat16), own_state[None].astype(jnp.bfloat16)),
                "grp",
                0,
                2,
            )
        )
    )
    group_index = jnp.arange(group_logs.shape[0])
    my_group = lax.axis_index("grp")
    inclusive = jnp.cumsum(group_logs, axis=0)
    exclusive = inclusive - group_logs
    before_me = jnp.sum(jnp.where((group_index == my_group)[:, None], exclusive, 0.0), axis=0)
    earlier_mask = (group_index < my_group)[:, None]
    weighting = jnp.where(
        earlier_mask, jnp.exp(jnp.where(earlier_mask, before_me[None, :] - inclusive, 0.0)), 0.0
    )
    entering = jnp.einsum("gh,ghpn->hpn", weighting, group_states, precision=HIGHEST_PREC)
    carried = jnp.exp(cumulative)[:, :, None] * jnp.einsum(
        "hpn,tn->thp", entering, out_float, precision=HIGHEST_PREC
    )
    ssm_out = inside + carried + skip_gain[None, :, None] * inputs_f
    gated_out = ssm_out.reshape(tok_rows, head_count * head_width) * jax.nn.silu(
        gate_input.astype(jnp.float32)
    )
    gated_gain = gated_out * norm_gain[None, :]
    squares = jnp.sum(gated_out * gated_out, axis=1)
    squares_hi = squares.astype(jnp.bfloat16)
    squares_lo = (squares - squares_hi.astype(jnp.float32)).astype(jnp.bfloat16)
    proj_rows = lax.all_to_all(
        out_proj.reshape(dev_count, -1, out_proj.shape[1]), DEV, 0, 0, tiled=True
    )
    partial = jnp.einsum(
        "tc,scf->tsf", gated_gain, proj_rows.astype(jnp.float32), precision=HIGHEST_PREC
    ).reshape(tok_rows, model_dim)
    lane_pad = jnp.zeros((tok_rows, 126), jnp.bfloat16)
    payload = jnp.concatenate(
        [partial.astype(jnp.bfloat16), squares_hi[:, None], squares_lo[:, None], lane_pad], axis=1
    )
    landed = lax.all_to_all(
        payload.reshape(dev_count, block_rows, payload.shape[1]), DEV, 0, 0, tiled=True
    ).astype(jnp.float32)
    summed_proj = jnp.sum(landed[:, :, :model_dim], axis=0)
    token_squares = jnp.sum(landed[:, :, model_dim] + landed[:, :, model_dim + 1], axis=0)
    mamba_out = (
        summed_proj * lax.rsqrt(token_squares / inner_dim + EPSILON)[:, None]
    ).astype(jnp.bfloat16)
    hidden_res = (residual.astype(jnp.float32) + mamba_out.astype(jnp.float32)).astype(jnp.bfloat16)
    hidden_float = hidden_res.astype(jnp.float32)
    normed = rms_scale(hidden_float, ffn_gain).astype(jnp.bfloat16)
    logits = jnp.dot(normed.astype(jnp.float32), router, precision=HIGHEST_PREC)
    expert_ids = jnp.arange(experts, dtype=jnp.int32)[None, :]
    first_logit = jnp.sum(logits * (routes[:, 0:1] == expert_ids).astype(jnp.float32), axis=1)
    second_logit = jnp.sum(logits * (routes[:, 1:2] == expert_ids).astype(jnp.float32), axis=1)
    first_prob = jax.nn.sigmoid(first_logit - second_logit)
    second_prob = 1.0 - first_prob
    placed = slot_tables(routes[None], experts, slot_cap)[0]
    filled = jnp.sum(placed, axis=1)
    outgoing = jnp.dot(
        filled.T.astype(jnp.bfloat16), normed, preferred_element_type=jnp.float32
    ).astype(jnp.bfloat16)
    outgoing = outgoing.reshape(experts, slot_cap, model_dim)
    arrived = lax.all_to_all(outgoing, "grp", split_axis=0, concat_axis=0, tiled=True)
    all_rows = ring_gather(ring_gather(arrived, "dev_1"), "dev_0").reshape(-1, model_dim)
    gate_act = jnp.dot(all_rows, gate_weight[0], preferred_element_type=jnp.float32)
    up_act = jnp.dot(all_rows, up_weight[0], preferred_element_type=jnp.float32)
    hidden = (jax.nn.silu(gate_act) * up_act).astype(jnp.bfloat16)
    partial_down = jnp.dot(hidden, down_weight[0], preferred_element_type=jnp.float32)
    spread_down = lax.all_to_all(
        partial_down.astype(jnp.bfloat16).reshape(dev_count, -1, model_dim), DEV, 0, 0, tiled=True
    )
    summed = jnp.sum(spread_down.astype(jnp.float32), axis=0)
    returned = lax.all_to_all(
        summed.astype(jnp.bfloat16).reshape(experts, slot_cap, model_dim),
        "grp",
        split_axis=0,
        concat_axis=0,
        tiled=True,
    )
    weights = first_prob[:, None] * placed[:, 0, :] + second_prob[:, None] * placed[:, 1, :]
    contrib = jnp.dot(
        weights,
        returned.reshape(group_slots, model_dim).astype(jnp.float32),
        precision=HIGHEST_PREC,
    )
    return (hidden_float + contrib).astype(jnp.bfloat16)


def solution(mesh):
    torus = Mesh(mesh.devices.reshape(mesh.shape["grp"], 4, 8), ("grp", "dev_0", "dev_1"))
    in_specs = (
        P("grp", DEV),
        P("grp", DEV),
        P("grp", DEV),
        P(DEV),
        P("grp", None),
        P("grp", None),
        P(DEV),
        P(DEV),
        P(None, DEV),
        P(GRP_DEV, None),
        P(),
        P(),
        P(GRP_DEV, None),
        P("grp", None, DEV),
        P("grp", None, DEV),
        P("grp", DEV, None),
    )
    out_specs = P(GRP_DEV, None)
    return jax.shard_map(
        shards, mesh=torus, in_specs=in_specs, out_specs=out_specs, check_vma=False
    )
```

```python
import jax
import jax.numpy as jnp
from jax import lax
from jax.sharding import Mesh
from jax.sharding import PartitionSpec as P

DEV = ("dev_0", "dev_1")
GRP_DEV = ("grp", "dev_0", "dev_1")


EPSILON = 1e-05
HIGHEST_PREC = lax.Precision.HIGHEST


def side_by_side(arrays, axis, dim, along):
    columns = [a.reshape(*a.shape[:along], -1) for a in arrays]
    both = jnp.concatenate(columns, axis=along)
    filled, at, finished = (lax.all_gather(both, axis, axis=dim, tiled=True), 0, [])
    for a, column in zip(arrays, columns):
        piece = filled[..., at : at + column.shape[along]]
        finished.append(piece.reshape(*piece.shape[:along], *a.shape[along:]))
        at += column.shape[along]
    return tuple(finished)


def sent_to_all(shard, axis):
    peers = lax.axis_size(axis)
    return lax.all_to_all(
        jnp.broadcast_to(shard[None], (peers, *shard.shape)), axis, 0, 0, tiled=True
    )


def of_everyone(shard, axis):
    everything = sent_to_all(shard, axis)
    return jnp.sum(everything, axis=0)


def in_order(tiles, dim):
    dims = list(tiles.shape[1:])
    dims[dim] *= tiles.shape[0]
    return jnp.moveaxis(tiles, 0, dim).reshape(dims)


def collect(shard, axis, dim):
    return in_order(sent_to_all(shard, axis), dim)


def sum_by_axis(terms, axes):
    total = terms.astype(jnp.bfloat16)
    for axis in axes:
        total = lax.psum_scatter(total, axis, scatter_dimension=0, tiled=True)
    return total.astype(jnp.float32)


def ring_gather(shard, axis):
    size = lax.axis_size(axis)
    forward, backward, pieces = shard, shard, {0: shard}
    for step in range(1, size // 2 + 1):
        forward = lax.ppermute(forward, axis, [(i, (i + 1) % size) for i in range(size)])
        pieces[-step] = forward
        if step < size - step:
            backward = lax.ppermute(backward, axis, [(i, (i - 1) % size) for i in range(size)])
            pieces[step] = backward
    offsets = list(range(-(size // 2), size - size // 2))
    stacked = jnp.stack([pieces[o] for o in offsets])
    doubled = jnp.concatenate([stacked, stacked])
    start = (-offsets[0] - lax.axis_index(axis)) % size
    return lax.dynamic_slice_in_dim(doubled, start, size, 0)


def rms_scale(values, gain_vec):
    return (
        values * lax.rsqrt(jnp.mean(values * values, axis=-1, keepdims=True) + EPSILON) * gain_vec
    )


def slot_tables(routes_block, expert_count, slot_cap):
    blocks, row_total = (routes_block.shape[0], routes_block.shape[1])
    flat_routes = routes_block.reshape(blocks, row_total * 2)
    onehot = (
        flat_routes[:, :, None] == jnp.arange(expert_count, dtype=jnp.int32)[None, None, :]
    ).astype(jnp.int32)
    earlier = jnp.cumsum(onehot, axis=1) - onehot
    slot_rank = jnp.sum(earlier * onehot, axis=2)
    slot_index = (flat_routes * slot_cap + slot_rank).reshape(blocks, row_total, 2)
    placed = (
        slot_index[:, :, :, None]
        == jnp.arange(expert_count * slot_cap, dtype=jnp.int32)[None, None, None, :]
    )
    return placed.astype(jnp.float32)


def shards(
    ssm_input,
    gate_input,
    step_size,
    decay_rate,
    in_coeff,
    out_coeff,
    skip_gain,
    norm_gain,
    out_proj,
    residual,
    ffn_gain,
    router,
    routes,
    gate_weight,
    up_weight,
    down_weight,
):
    tok_rows = ssm_input.shape[0]
    head_count = step_size.shape[1]
    head_width = ssm_input.shape[1] // head_count
    dev_count = lax.axis_size(DEV)
    inner_dim = ssm_input.shape[1] * dev_count
    block_rows = residual.shape[0]
    model_dim = residual.shape[1]
    experts = lax.axis_size("grp")
    slot_cap = max(2, 4 * block_rows // experts)
    group_slots = experts * slot_cap
    inputs_f = ssm_input.astype(jnp.float32).reshape(tok_rows, head_count, head_width)
    in_float = in_coeff.astype(jnp.float32)
    out_float = out_coeff.astype(jnp.float32)
    log_rate = -(step_size * decay_rate[None, :])
    cumulative = jnp.cumsum(log_rate, axis=0)
    causal = (jnp.arange(tok_rows)[:, None] >= jnp.arange(tok_rows)[None, :])[:, :, None]
    spread = cumulative[:, None, :] - cumulative[None, :, :]
    decay_pair = jnp.where(causal, jnp.exp(jnp.where(causal, spread, 0.0)), 0.0)
    scores = jnp.dot(out_coeff, in_coeff.T, preferred_element_type=jnp.float32)
    mixing = decay_pair * scores[:, :, None] * step_size[None, :, :]
    inside = jnp.einsum("tuh,uhp->thp", mixing, inputs_f, precision=HIGHEST_PREC)
    to_end = jnp.exp(cumulative[-1][None, :] - cumulative) * step_size
    own_state = jnp.einsum("uh,uhp,un->hpn", to_end, inputs_f, in_float, precision=HIGHEST_PREC)
    own_log = cumulative[-1]
    group_logs, group_states = tuple(
        (
            part.astype(jnp.float32)
            for part in side_by_side(
                (own_log[None].astype(jnp.bfloat16), own_state[None].astype(jnp.bfloat16)),
                "grp",
                0,
                2,
            )
        )
    )
    group_index = jnp.arange(group_logs.shape[0])
    my_group = lax.axis_index("grp")
    inclusive = jnp.cumsum(group_logs, axis=0)
    exclusive = inclusive - group_logs
    before_me = jnp.sum(jnp.where((group_index == my_group)[:, None], exclusive, 0.0), axis=0)
    earlier_mask = (group_index < my_group)[:, None]
    weighting = jnp.where(
        earlier_mask, jnp.exp(jnp.where(earlier_mask, before_me[None, :] - inclusive, 0.0)), 0.0
    )
    entering = jnp.einsum("gh,ghpn->hpn", weighting, group_states, precision=HIGHEST_PREC)
    carried = jnp.exp(cumulative)[:, :, None] * jnp.einsum(
        "hpn,tn->thp", entering, out_float, precision=HIGHEST_PREC
    )
    ssm_out = inside + carried + skip_gain[None, :, None] * inputs_f
    gated_out = ssm_out.reshape(tok_rows, head_count * head_width) * jax.nn.silu(
        gate_input.astype(jnp.float32)
    )
    gated_gain = gated_out * norm_gain[None, :]
    squares = gated_out * gated_out
    proj_rows = lax.all_to_all(
        out_proj.reshape(dev_count, -1, out_proj.shape[1]), DEV, 0, 0, tiled=True
    )
    chan = proj_rows.shape[1]
    proj_rows = jnp.transpose(proj_rows, (1, 0, 2)).reshape(chan, model_dim)
    lane_pad = 128
    square_cols = (jnp.arange(lane_pad) == 0).astype(jnp.bfloat16)
    rhs = jnp.concatenate(
        [
            jnp.concatenate([proj_rows, jnp.zeros((chan, lane_pad), jnp.bfloat16)], axis=1),
            jnp.concatenate(
                [jnp.zeros((chan, model_dim), jnp.bfloat16), jnp.broadcast_to(square_cols, (chan, lane_pad))],
                axis=1,
            ),
        ],
        axis=0,
    )
    lhs = jnp.concatenate([gated_gain, squares], axis=1).astype(jnp.bfloat16)
    payload = jnp.dot(lhs, rhs, preferred_element_type=jnp.float32).astype(jnp.bfloat16)
    landed = lax.all_to_all(
        payload.reshape(dev_count, block_rows, payload.shape[1]), DEV, 0, 0, tiled=True
    ).astype(jnp.float32)
    summed_proj = jnp.sum(landed[:, :, :model_dim], axis=0)
    token_squares = jnp.sum(landed[:, :, model_dim], axis=0)
    mamba_out = (
        summed_proj * lax.rsqrt(token_squares / inner_dim + EPSILON)[:, None]
    ).astype(jnp.bfloat16)
    hidden_res = (residual.astype(jnp.float32) + mamba_out.astype(jnp.float32)).astype(jnp.bfloat16)
    hidden_float = hidden_res.astype(jnp.float32)
    normed = rms_scale(hidden_float, ffn_gain).astype(jnp.bfloat16)
    logits = jnp.dot(normed.astype(jnp.float32), router, precision=HIGHEST_PREC)
    expert_ids = jnp.arange(experts, dtype=jnp.int32)[None, :]
    first_logit = jnp.sum(logits * (routes[:, 0:1] == expert_ids).astype(jnp.float32), axis=1)
    second_logit = jnp.sum(logits * (routes[:, 1:2] == expert_ids).astype(jnp.float32), axis=1)
    first_prob = jax.nn.sigmoid(first_logit - second_logit)
    second_prob = 1.0 - first_prob
    placed = slot_tables(routes[None], experts, slot_cap)[0]
    filled = jnp.sum(placed, axis=1)
    outgoing = jnp.dot(
        filled.T.astype(jnp.bfloat16), normed, preferred_element_type=jnp.float32
    ).astype(jnp.bfloat16)
    outgoing = outgoing.reshape(experts, slot_cap, model_dim)
    arrived = lax.all_to_all(outgoing, "grp", split_axis=0, concat_axis=0, tiled=True)
    all_rows = arrived.reshape(-1, model_dim)
    all_rows = lax.all_gather(all_rows, "dev_0", axis=0, tiled=True)
    all_rows = lax.all_gather(all_rows, "dev_1", axis=0, tiled=True)
    gate_act = jnp.dot(all_rows, gate_weight[0], preferred_element_type=jnp.float32)
    up_act = jnp.dot(all_rows, up_weight[0], preferred_element_type=jnp.float32)
    hidden = (jax.nn.silu(gate_act) * up_act).astype(jnp.bfloat16)
    partial_down = jnp.dot(hidden, down_weight[0], preferred_element_type=jnp.float32)
    summed = lax.psum_scatter(
        partial_down.astype(jnp.bfloat16), "dev_1", scatter_dimension=0, tiled=True
    )
    summed = lax.psum_scatter(summed, "dev_0", scatter_dimension=0, tiled=True)
    returned = lax.all_to_all(
        summed.astype(jnp.bfloat16).reshape(experts, slot_cap, model_dim),
        "grp",
        split_axis=0,
        concat_axis=0,
        tiled=True,
    )
    weights = first_prob[:, None] * placed[:, 0, :] + second_prob[:, None] * placed[:, 1, :]
    contrib = jnp.dot(
        weights,
        returned.reshape(group_slots, model_dim).astype(jnp.float32),
        precision=HIGHEST_PREC,
    )
    return (hidden_float + contrib).astype(jnp.bfloat16)


def solution(mesh):
    torus = Mesh(mesh.devices.reshape(mesh.shape["grp"], 4, 8), ("grp", "dev_0", "dev_1"))
    in_specs = (
        P("grp", DEV),
        P("grp", DEV),
        P("grp", DEV),
        P(DEV),
        P("grp", None),
        P("grp", None),
        P(DEV),
        P(DEV),
        P(None, DEV),
        P(GRP_DEV, None),
        P(),
        P(),
        P(GRP_DEV, None),
        P("grp", None, DEV),
        P("grp", None, DEV),
        P("grp", DEV, None),
    )
    out_specs = P(GRP_DEV, None)
    return jax.shard_map(
        shards, mesh=torus, in_specs=in_specs, out_specs=out_specs, check_vma=False
    )
```

```python
import jax
import jax.numpy as jnp
from jax import lax
from jax.sharding import Mesh
from jax.sharding import PartitionSpec as P

DEV = ("dev_0", "dev_1")
GRP_DEV = ("grp", "dev_0", "dev_1")


EPSILON = 1e-05
HIGHEST_PREC = lax.Precision.HIGHEST


def side_by_side(arrays, axis, dim, along):
    columns = [a.reshape(*a.shape[:along], -1) for a in arrays]
    both = jnp.concatenate(columns, axis=along)
    filled, at, finished = (lax.all_gather(both, axis, axis=dim, tiled=True), 0, [])
    for a, column in zip(arrays, columns):
        piece = filled[..., at : at + column.shape[along]]
        finished.append(piece.reshape(*piece.shape[:along], *a.shape[along:]))
        at += column.shape[along]
    return tuple(finished)


def sent_to_all(shard, axis):
    peers = lax.axis_size(axis)
    return lax.all_to_all(
        jnp.broadcast_to(shard[None], (peers, *shard.shape)), axis, 0, 0, tiled=True
    )


def of_everyone(shard, axis):
    everything = sent_to_all(shard, axis)
    return jnp.sum(everything, axis=0)


def in_order(tiles, dim):
    dims = list(tiles.shape[1:])
    dims[dim] *= tiles.shape[0]
    return jnp.moveaxis(tiles, 0, dim).reshape(dims)


def collect(shard, axis, dim):
    return in_order(sent_to_all(shard, axis), dim)


def sum_by_axis(terms, axes):
    total = terms.astype(jnp.bfloat16)
    for axis in axes:
        total = lax.psum_scatter(total, axis, scatter_dimension=0, tiled=True)
    return total.astype(jnp.float32)


def ring_gather(shard, axis):
    size = lax.axis_size(axis)
    forward, backward, pieces = shard, shard, {0: shard}
    for step in range(1, size // 2 + 1):
        forward = lax.ppermute(forward, axis, [(i, (i + 1) % size) for i in range(size)])
        pieces[-step] = forward
        if step < size - step:
            backward = lax.ppermute(backward, axis, [(i, (i - 1) % size) for i in range(size)])
            pieces[step] = backward
    offsets = list(range(-(size // 2), size - size // 2))
    stacked = jnp.stack([pieces[o] for o in offsets])
    doubled = jnp.concatenate([stacked, stacked])
    start = (-offsets[0] - lax.axis_index(axis)) % size
    return lax.dynamic_slice_in_dim(doubled, start, size, 0)


def rms_scale(values, gain_vec):
    return (
        values * lax.rsqrt(jnp.mean(values * values, axis=-1, keepdims=True) + EPSILON) * gain_vec
    )


def slot_tables(routes_block, expert_count, slot_cap):
    blocks, row_total = (routes_block.shape[0], routes_block.shape[1])
    flat_routes = routes_block.reshape(blocks, row_total * 2)
    onehot = (
        flat_routes[:, :, None] == jnp.arange(expert_count, dtype=jnp.int32)[None, None, :]
    ).astype(jnp.int32)
    earlier = jnp.cumsum(onehot, axis=1) - onehot
    slot_rank = jnp.sum(earlier * onehot, axis=2)
    slot_index = (flat_routes * slot_cap + slot_rank).reshape(blocks, row_total, 2)
    placed = (
        slot_index[:, :, :, None]
        == jnp.arange(expert_count * slot_cap, dtype=jnp.int32)[None, None, None, :]
    )
    return placed.astype(jnp.float32)


def shards(
    ssm_input,
    gate_input,
    step_size,
    decay_rate,
    in_coeff,
    out_coeff,
    skip_gain,
    norm_gain,
    out_proj,
    residual,
    ffn_gain,
    router,
    routes,
    gate_weight,
    up_weight,
    down_weight,
):
    tok_rows = ssm_input.shape[0]
    head_count = step_size.shape[1]
    head_width = ssm_input.shape[1] // head_count
    dev_count = lax.axis_size(DEV)
    inner_dim = ssm_input.shape[1] * dev_count
    block_rows = residual.shape[0]
    model_dim = residual.shape[1]
    experts = lax.axis_size("grp")
    slot_cap = max(2, 4 * block_rows // experts)
    group_slots = experts * slot_cap
    inputs_f = ssm_input.astype(jnp.float32).reshape(tok_rows, head_count, head_width)
    in_float = in_coeff.astype(jnp.float32)
    out_float = out_coeff.astype(jnp.float32)
    log_rate = -(step_size * decay_rate[None, :])
    cumulative = jnp.cumsum(log_rate, axis=0)
    causal = (jnp.arange(tok_rows)[:, None] >= jnp.arange(tok_rows)[None, :])[:, :, None]
    spread = cumulative[:, None, :] - cumulative[None, :, :]
    decay_pair = jnp.where(causal, jnp.exp(jnp.where(causal, spread, 0.0)), 0.0)
    scores = jnp.dot(out_coeff, in_coeff.T, preferred_element_type=jnp.float32)
    mixing = decay_pair * scores[:, :, None] * step_size[None, :, :]
    inside = jnp.einsum("tuh,uhp->thp", mixing, inputs_f, precision=HIGHEST_PREC)
    to_end = jnp.exp(cumulative[-1][None, :] - cumulative) * step_size
    own_state = jnp.einsum("uh,uhp,un->hpn", to_end, inputs_f, in_float, precision=HIGHEST_PREC)
    own_log = cumulative[-1]
    group_logs, group_states = tuple(
        (
            part.astype(jnp.float32)
            for part in side_by_side(
                (own_log[None].astype(jnp.bfloat16), own_state[None].astype(jnp.bfloat16)),
                "grp",
                0,
                2,
            )
        )
    )
    group_index = jnp.arange(group_logs.shape[0])
    my_group = lax.axis_index("grp")
    inclusive = jnp.cumsum(group_logs, axis=0)
    exclusive = inclusive - group_logs
    before_me = jnp.sum(jnp.where((group_index == my_group)[:, None], exclusive, 0.0), axis=0)
    earlier_mask = (group_index < my_group)[:, None]
    weighting = jnp.where(
        earlier_mask, jnp.exp(jnp.where(earlier_mask, before_me[None, :] - inclusive, 0.0)), 0.0
    )
    entering = jnp.einsum("gh,ghpn->hpn", weighting, group_states, precision=HIGHEST_PREC)
    carried = jnp.exp(cumulative)[:, :, None] * jnp.einsum(
        "hpn,tn->thp", entering, out_float, precision=HIGHEST_PREC
    )
    ssm_out = inside + carried + skip_gain[None, :, None] * inputs_f
    gated_out = ssm_out.reshape(tok_rows, head_count * head_width) * jax.nn.silu(
        gate_input.astype(jnp.float32)
    )
    gated_gain = gated_out * norm_gain[None, :]
    squares = gated_out * gated_out
    proj_rows = lax.all_to_all(
        out_proj.reshape(dev_count, -1, out_proj.shape[1]), DEV, 0, 0, tiled=True
    )
    chan = proj_rows.shape[1]
    proj_rows = jnp.transpose(proj_rows, (1, 0, 2)).reshape(chan, model_dim)
    lane_pad = 128
    square_cols = (jnp.arange(lane_pad) == 0).astype(jnp.bfloat16)
    rhs = jnp.concatenate(
        [
            jnp.concatenate([proj_rows, jnp.zeros((chan, lane_pad), jnp.bfloat16)], axis=1),
            jnp.concatenate(
                [jnp.zeros((chan, model_dim), jnp.bfloat16), jnp.broadcast_to(square_cols, (chan, lane_pad))],
                axis=1,
            ),
        ],
        axis=0,
    )
    lhs = jnp.concatenate([gated_gain, squares], axis=1).astype(jnp.bfloat16)
    payload = jnp.dot(lhs, rhs, preferred_element_type=jnp.float32).astype(jnp.bfloat16)
    landed = lax.all_to_all(
        payload.reshape(dev_count, block_rows, payload.shape[1]), DEV, 0, 0, tiled=True
    ).astype(jnp.float32)
    summed_proj = jnp.sum(landed[:, :, :model_dim], axis=0)
    token_squares = jnp.sum(landed[:, :, model_dim], axis=0)
    mamba_out = (
        summed_proj * lax.rsqrt(token_squares / inner_dim + EPSILON)[:, None]
    ).astype(jnp.bfloat16)
    hidden_res = (residual.astype(jnp.float32) + mamba_out.astype(jnp.float32)).astype(jnp.bfloat16)
    hidden_float = hidden_res.astype(jnp.float32)
    normed = rms_scale(hidden_float, ffn_gain).astype(jnp.bfloat16)
    logits = jnp.dot(normed.astype(jnp.float32), router, precision=HIGHEST_PREC)
    expert_ids = jnp.arange(experts, dtype=jnp.int32)[None, :]
    first_logit = jnp.sum(logits * (routes[:, 0:1] == expert_ids).astype(jnp.float32), axis=1)
    second_logit = jnp.sum(logits * (routes[:, 1:2] == expert_ids).astype(jnp.float32), axis=1)
    first_prob = jax.nn.sigmoid(first_logit - second_logit)
    second_prob = 1.0 - first_prob
    placed = slot_tables(routes[None], experts, slot_cap)[0]
    filled = jnp.sum(placed, axis=1)
    outgoing = jnp.dot(
        filled.T.astype(jnp.bfloat16), normed, preferred_element_type=jnp.float32
    ).astype(jnp.bfloat16)
    outgoing = outgoing.reshape(experts, slot_cap, model_dim)
    arrived = lax.all_to_all(outgoing, "grp", split_axis=0, concat_axis=0, tiled=True)
    all_rows = arrived.reshape(-1, model_dim)
    all_rows = lax.all_gather(all_rows, "dev_0", axis=0, tiled=True)
    all_rows = lax.all_gather(all_rows, "dev_1", axis=0, tiled=True)
    gate_act = jnp.dot(all_rows, gate_weight[0], preferred_element_type=jnp.float32)
    up_act = jnp.dot(all_rows, up_weight[0], preferred_element_type=jnp.float32)
    hidden = (jax.nn.silu(gate_act) * up_act).astype(jnp.bfloat16)
    partial_down = jnp.dot(hidden, down_weight[0], preferred_element_type=jnp.float32)
    summed = lax.psum_scatter(
        partial_down.astype(jnp.bfloat16), "dev_1", scatter_dimension=0, tiled=True
    )
    x_count = lax.axis_size("dev_0")
    summed = jnp.swapaxes(summed.reshape(x_count, experts, slot_cap, model_dim), 0, 1)
    landed_back = lax.all_to_all(
        summed.reshape(experts * x_count, slot_cap, model_dim), ("grp", "dev_0"), 0, 0, tiled=True
    )
    returned = jnp.sum(
        landed_back.reshape(experts, x_count, slot_cap, model_dim).astype(jnp.float32), axis=1
    )
    weights = first_prob[:, None] * placed[:, 0, :] + second_prob[:, None] * placed[:, 1, :]
    contrib = jnp.dot(
        weights,
        returned.reshape(group_slots, model_dim),
        precision=HIGHEST_PREC,
    )
    return (hidden_float + contrib).astype(jnp.bfloat16)


def solution(mesh):
    torus = Mesh(mesh.devices.reshape(mesh.shape["grp"], 4, 8), ("grp", "dev_0", "dev_1"))
    in_specs = (
        P("grp", DEV),
        P("grp", DEV),
        P("grp", DEV),
        P(DEV),
        P("grp", None),
        P("grp", None),
        P(DEV),
        P(DEV),
        P(None, DEV),
        P(GRP_DEV, None),
        P(),
        P(),
        P(GRP_DEV, None),
        P("grp", None, DEV),
        P("grp", None, DEV),
        P("grp", DEV, None),
    )
    out_specs = P(GRP_DEV, None)
    return jax.shard_map(
        shards, mesh=torus, in_specs=in_specs, out_specs=out_specs, check_vma=False
    )
```

```python
import jax
import jax.numpy as jnp
from jax import lax
from jax.sharding import Mesh
from jax.sharding import PartitionSpec as P

DEV = ("dev_0", "dev_1")
GRP_DEV = ("grp", "dev_0", "dev_1")


EPSILON = 1e-05
HIGHEST_PREC = lax.Precision.HIGHEST


def side_by_side(arrays, axis, dim, along):
    columns = [a.reshape(*a.shape[:along], -1) for a in arrays]
    both = jnp.concatenate(columns, axis=along)
    filled, at, finished = (lax.all_gather(both, axis, axis=dim, tiled=True), 0, [])
    for a, column in zip(arrays, columns):
        piece = filled[..., at : at + column.shape[along]]
        finished.append(piece.reshape(*piece.shape[:along], *a.shape[along:]))
        at += column.shape[along]
    return tuple(finished)


def sent_to_all(shard, axis):
    peers = lax.axis_size(axis)
    return lax.all_to_all(
        jnp.broadcast_to(shard[None], (peers, *shard.shape)), axis, 0, 0, tiled=True
    )


def of_everyone(shard, axis):
    everything = sent_to_all(shard, axis)
    return jnp.sum(everything, axis=0)


def in_order(tiles, dim):
    dims = list(tiles.shape[1:])
    dims[dim] *= tiles.shape[0]
    return jnp.moveaxis(tiles, 0, dim).reshape(dims)


def collect(shard, axis, dim):
    return in_order(sent_to_all(shard, axis), dim)


def sum_by_axis(terms, axes):
    total = terms.astype(jnp.bfloat16)
    for axis in axes:
        total = lax.psum_scatter(total, axis, scatter_dimension=0, tiled=True)
    return total.astype(jnp.float32)


def ring_gather(shard, axis):
    size = lax.axis_size(axis)
    forward, backward, pieces = shard, shard, {0: shard}
    for step in range(1, size // 2 + 1):
        forward = lax.ppermute(forward, axis, [(i, (i + 1) % size) for i in range(size)])
        pieces[-step] = forward
        if step < size - step:
            backward = lax.ppermute(backward, axis, [(i, (i - 1) % size) for i in range(size)])
            pieces[step] = backward
    offsets = list(range(-(size // 2), size - size // 2))
    stacked = jnp.stack([pieces[o] for o in offsets])
    doubled = jnp.concatenate([stacked, stacked])
    start = (-offsets[0] - lax.axis_index(axis)) % size
    return lax.dynamic_slice_in_dim(doubled, start, size, 0)


def rms_scale(values, gain_vec):
    return (
        values * lax.rsqrt(jnp.mean(values * values, axis=-1, keepdims=True) + EPSILON) * gain_vec
    )


def slot_tables(routes_block, expert_count, slot_cap):
    blocks, row_total = (routes_block.shape[0], routes_block.shape[1])
    flat_routes = routes_block.reshape(blocks, row_total * 2)
    onehot = (
        flat_routes[:, :, None] == jnp.arange(expert_count, dtype=jnp.int32)[None, None, :]
    ).astype(jnp.int32)
    earlier = jnp.cumsum(onehot, axis=1) - onehot
    slot_rank = jnp.sum(earlier * onehot, axis=2)
    slot_index = (flat_routes * slot_cap + slot_rank).reshape(blocks, row_total, 2)
    placed = (
        slot_index[:, :, :, None]
        == jnp.arange(expert_count * slot_cap, dtype=jnp.int32)[None, None, None, :]
    )
    return placed.astype(jnp.float32)


def shards(
    ssm_input,
    gate_input,
    step_size,
    decay_rate,
    in_coeff,
    out_coeff,
    skip_gain,
    norm_gain,
    out_proj,
    residual,
    ffn_gain,
    router,
    routes,
    gate_weight,
    up_weight,
    down_weight,
):
    tok_rows = ssm_input.shape[0]
    head_count = step_size.shape[1]
    head_width = ssm_input.shape[1] // head_count
    dev_count = lax.axis_size(DEV)
    inner_dim = ssm_input.shape[1] * dev_count
    block_rows = residual.shape[0]
    model_dim = residual.shape[1]
    experts = lax.axis_size("grp")
    slot_cap = max(2, 4 * block_rows // experts)
    group_slots = experts * slot_cap
    inputs_f = ssm_input.astype(jnp.float32).reshape(tok_rows, head_count, head_width)
    in_float = in_coeff.astype(jnp.float32)
    out_float = out_coeff.astype(jnp.float32)
    log_rate = -(step_size * decay_rate[None, :])
    cumulative = jnp.cumsum(log_rate, axis=0)
    causal = (jnp.arange(tok_rows)[:, None] >= jnp.arange(tok_rows)[None, :])[:, :, None]
    spread = cumulative[:, None, :] - cumulative[None, :, :]
    decay_pair = jnp.where(causal, jnp.exp(jnp.where(causal, spread, 0.0)), 0.0)
    scores = jnp.dot(out_coeff, in_coeff.T, preferred_element_type=jnp.float32)
    mixing = decay_pair * scores[:, :, None] * step_size[None, :, :]
    inside = jnp.einsum("tuh,uhp->thp", mixing, inputs_f, precision=HIGHEST_PREC)
    to_end = jnp.exp(cumulative[-1][None, :] - cumulative) * step_size
    own_state = jnp.einsum("uh,uhp,un->hpn", to_end, inputs_f, in_float, precision=HIGHEST_PREC)
    own_log = cumulative[-1]
    group_logs, group_states = tuple(
        (
            part.astype(jnp.float32)
            for part in side_by_side(
                (own_log[None].astype(jnp.bfloat16), own_state[None].astype(jnp.bfloat16)),
                "grp",
                0,
                2,
            )
        )
    )
    group_index = jnp.arange(group_logs.shape[0])
    my_group = lax.axis_index("grp")
    inclusive = jnp.cumsum(group_logs, axis=0)
    exclusive = inclusive - group_logs
    before_me = jnp.sum(jnp.where((group_index == my_group)[:, None], exclusive, 0.0), axis=0)
    earlier_mask = (group_index < my_group)[:, None]
    weighting = jnp.where(
        earlier_mask, jnp.exp(jnp.where(earlier_mask, before_me[None, :] - inclusive, 0.0)), 0.0
    )
    entering = jnp.einsum("gh,ghpn->hpn", weighting, group_states, precision=HIGHEST_PREC)
    carried = jnp.exp(cumulative)[:, :, None] * jnp.einsum(
        "hpn,tn->thp", entering, out_float, precision=HIGHEST_PREC
    )
    ssm_out = inside + carried + skip_gain[None, :, None] * inputs_f
    gated_out = ssm_out.reshape(tok_rows, head_count * head_width) * jax.nn.silu(
        gate_input.astype(jnp.float32)
    )
    gated_gain = gated_out * norm_gain[None, :]
    squares = gated_out * gated_out
    proj_rows = lax.all_to_all(
        out_proj.reshape(dev_count, -1, out_proj.shape[1]), DEV, 0, 0, tiled=True
    )
    chan = proj_rows.shape[1]
    proj_rows = jnp.transpose(proj_rows, (1, 0, 2)).reshape(chan, model_dim)
    lane_pad = 128
    square_cols = (jnp.arange(lane_pad) == 0).astype(jnp.bfloat16)
    rhs = jnp.concatenate(
        [
            jnp.concatenate([proj_rows, jnp.zeros((chan, lane_pad), jnp.bfloat16)], axis=1),
            jnp.concatenate(
                [jnp.zeros((chan, model_dim), jnp.bfloat16), jnp.broadcast_to(square_cols, (chan, lane_pad))],
                axis=1,
            ),
        ],
        axis=0,
    )
    lhs = jnp.concatenate([gated_gain, squares], axis=1).astype(jnp.bfloat16)
    payload = jnp.dot(lhs, rhs, preferred_element_type=jnp.float32).astype(jnp.bfloat16)
    landed = lax.all_to_all(
        payload.reshape(dev_count, block_rows, payload.shape[1]), DEV, 0, 0, tiled=True
    ).astype(jnp.float32)
    summed_proj = jnp.sum(landed[:, :, :model_dim], axis=0)
    token_squares = jnp.sum(landed[:, :, model_dim], axis=0)
    mamba_out = (
        summed_proj * lax.rsqrt(token_squares / inner_dim + EPSILON)[:, None]
    ).astype(jnp.bfloat16)
    hidden_res = (residual.astype(jnp.float32) + mamba_out.astype(jnp.float32)).astype(jnp.bfloat16)
    hidden_float = hidden_res.astype(jnp.float32)
    normed = rms_scale(hidden_float, ffn_gain).astype(jnp.bfloat16)
    logits = jnp.dot(normed.astype(jnp.float32), router, precision=HIGHEST_PREC)
    expert_ids = jnp.arange(experts, dtype=jnp.int32)[None, :]
    first_logit = jnp.sum(logits * (routes[:, 0:1] == expert_ids).astype(jnp.float32), axis=1)
    second_logit = jnp.sum(logits * (routes[:, 1:2] == expert_ids).astype(jnp.float32), axis=1)
    first_prob = jax.nn.sigmoid(first_logit - second_logit)
    second_prob = 1.0 - first_prob
    placed = slot_tables(routes[None], experts, slot_cap)[0]
    filled = jnp.sum(placed, axis=1)
    outgoing = jnp.dot(
        filled.T.astype(jnp.bfloat16), normed, preferred_element_type=jnp.float32
    ).astype(jnp.bfloat16)
    outgoing = outgoing.reshape(experts, slot_cap, model_dim)
    arrived = lax.all_to_all(outgoing, "grp", split_axis=0, concat_axis=0, tiled=True)
    x_count = lax.axis_size("dev_0")
    halves = []
    for slot in range(slot_cap):
        rows = lax.all_gather(arrived[:, slot, :], "dev_0", axis=0, tiled=True)
        rows = lax.all_gather(rows, "dev_1", axis=0, tiled=True)
        gate_act = jnp.dot(rows, gate_weight[0], preferred_element_type=jnp.float32)
        up_act = jnp.dot(rows, up_weight[0], preferred_element_type=jnp.float32)
        hidden = (jax.nn.silu(gate_act) * up_act).astype(jnp.bfloat16)
        partial_down = jnp.dot(hidden, down_weight[0], preferred_element_type=jnp.float32)
        summed = lax.psum_scatter(
            partial_down.astype(jnp.bfloat16), "dev_1", scatter_dimension=0, tiled=True
        )
        summed = jnp.swapaxes(summed.reshape(x_count, experts, model_dim), 0, 1)
        landed_back = lax.all_to_all(
            summed.reshape(experts * x_count, model_dim), ("grp", "dev_0"), 0, 0, tiled=True
        )
        halves.append(
            jnp.sum(landed_back.reshape(experts, x_count, model_dim).astype(jnp.float32), axis=1)
        )
    returned = jnp.stack(halves, axis=1)
    weights = first_prob[:, None] * placed[:, 0, :] + second_prob[:, None] * placed[:, 1, :]
    contrib = jnp.dot(
        weights,
        returned.reshape(group_slots, model_dim),
        precision=HIGHEST_PREC,
    )
    return (hidden_float + contrib).astype(jnp.bfloat16)


def solution(mesh):
    torus = Mesh(mesh.devices.reshape(mesh.shape["grp"], 4, 8), ("grp", "dev_0", "dev_1"))
    in_specs = (
        P("grp", DEV),
        P("grp", DEV),
        P("grp", DEV),
        P(DEV),
        P("grp", None),
        P("grp", None),
        P(DEV),
        P(DEV),
        P(None, DEV),
        P(GRP_DEV, None),
        P(),
        P(),
        P(GRP_DEV, None),
        P("grp", None, DEV),
        P("grp", None, DEV),
        P("grp", DEV, None),
    )
    out_specs = P(GRP_DEV, None)
    return jax.shard_map(
        shards, mesh=torus, in_specs=in_specs, out_specs=out_specs, check_vma=False
    )
```

```python
import jax
import jax.numpy as jnp
from jax import lax
from jax.sharding import Mesh
from jax.sharding import PartitionSpec as P

DEV = ("dev_0", "dev_1")
GRP_DEV = ("grp", "dev_0", "dev_1")


EPSILON = 1e-05
HIGHEST_PREC = lax.Precision.HIGHEST


def side_by_side(arrays, axis, dim, along):
    columns = [a.reshape(*a.shape[:along], -1) for a in arrays]
    both = jnp.concatenate(columns, axis=along)
    filled, at, finished = (lax.all_gather(both, axis, axis=dim, tiled=True), 0, [])
    for a, column in zip(arrays, columns):
        piece = filled[..., at : at + column.shape[along]]
        finished.append(piece.reshape(*piece.shape[:along], *a.shape[along:]))
        at += column.shape[along]
    return tuple(finished)


def sent_to_all(shard, axis):
    peers = lax.axis_size(axis)
    return lax.all_to_all(
        jnp.broadcast_to(shard[None], (peers, *shard.shape)), axis, 0, 0, tiled=True
    )


def of_everyone(shard, axis):
    everything = sent_to_all(shard, axis)
    return jnp.sum(everything, axis=0)


def in_order(tiles, dim):
    dims = list(tiles.shape[1:])
    dims[dim] *= tiles.shape[0]
    return jnp.moveaxis(tiles, 0, dim).reshape(dims)


def collect(shard, axis, dim):
    return in_order(sent_to_all(shard, axis), dim)


def sum_by_axis(terms, axes):
    total = terms.astype(jnp.bfloat16)
    for axis in axes:
        total = lax.psum_scatter(total, axis, scatter_dimension=0, tiled=True)
    return total.astype(jnp.float32)


def ring_gather(shard, axis):
    size = lax.axis_size(axis)
    forward, backward, pieces = shard, shard, {0: shard}
    for step in range(1, size // 2 + 1):
        forward = lax.ppermute(forward, axis, [(i, (i + 1) % size) for i in range(size)])
        pieces[-step] = forward
        if step < size - step:
            backward = lax.ppermute(backward, axis, [(i, (i - 1) % size) for i in range(size)])
            pieces[step] = backward
    offsets = list(range(-(size // 2), size - size // 2))
    stacked = jnp.stack([pieces[o] for o in offsets])
    doubled = jnp.concatenate([stacked, stacked])
    start = (-offsets[0] - lax.axis_index(axis)) % size
    return lax.dynamic_slice_in_dim(doubled, start, size, 0)


def ring_pieces(shard, axis):
    size = lax.axis_size(axis)
    forward, backward, pieces = shard, shard, [shard]
    for step in range(1, size // 2 + 1):
        forward = lax.ppermute(forward, axis, [(i, (i + 1) % size) for i in range(size)])
        pieces.append(forward)
        if step < size - step:
            backward = lax.ppermute(backward, axis, [(i, (i - 1) % size) for i in range(size)])
            pieces.append(backward)
    return pieces


def rms_scale(values, gain_vec):
    return (
        values * lax.rsqrt(jnp.mean(values * values, axis=-1, keepdims=True) + EPSILON) * gain_vec
    )


def slot_tables(routes_block, expert_count, slot_cap):
    blocks, row_total = (routes_block.shape[0], routes_block.shape[1])
    flat_routes = routes_block.reshape(blocks, row_total * 2)
    onehot = (
        flat_routes[:, :, None] == jnp.arange(expert_count, dtype=jnp.int32)[None, None, :]
    ).astype(jnp.int32)
    earlier = jnp.cumsum(onehot, axis=1) - onehot
    slot_rank = jnp.sum(earlier * onehot, axis=2)
    slot_index = (flat_routes * slot_cap + slot_rank).reshape(blocks, row_total, 2)
    placed = (
        slot_index[:, :, :, None]
        == jnp.arange(expert_count * slot_cap, dtype=jnp.int32)[None, None, None, :]
    )
    return placed.astype(jnp.float32)


def shards(
    ssm_input,
    gate_input,
    step_size,
    decay_rate,
    in_coeff,
    out_coeff,
    skip_gain,
    norm_gain,
    out_proj,
    residual,
    ffn_gain,
    router,
    routes,
    gate_weight,
    up_weight,
    down_weight,
):
    tok_rows = ssm_input.shape[0]
    head_count = step_size.shape[1]
    head_width = ssm_input.shape[1] // head_count
    dev_count = lax.axis_size(DEV)
    inner_dim = ssm_input.shape[1] * dev_count
    block_rows = residual.shape[0]
    model_dim = residual.shape[1]
    experts = lax.axis_size("grp")
    slot_cap = max(2, 4 * block_rows // experts)
    group_slots = experts * slot_cap
    x_count = lax.axis_size("dev_0")
    own_w = jnp.stack([gate_weight[0], up_weight[0], down_weight[0].T])
    expert_w = ring_pieces(own_w, "dev_0")
    inputs_f = ssm_input.astype(jnp.float32).reshape(tok_rows, head_count, head_width)
    in_float = in_coeff.astype(jnp.float32)
    out_float = out_coeff.astype(jnp.float32)
    log_rate = -(step_size * decay_rate[None, :])
    cumulative = jnp.cumsum(log_rate, axis=0)
    causal = (jnp.arange(tok_rows)[:, None] >= jnp.arange(tok_rows)[None, :])[:, :, None]
    spread = cumulative[:, None, :] - cumulative[None, :, :]
    decay_pair = jnp.where(causal, jnp.exp(jnp.where(causal, spread, 0.0)), 0.0)
    scores = jnp.dot(out_coeff, in_coeff.T, preferred_element_type=jnp.float32)
    mixing = decay_pair * scores[:, :, None] * step_size[None, :, :]
    inside = jnp.einsum("tuh,uhp->thp", mixing, inputs_f, precision=HIGHEST_PREC)
    to_end = jnp.exp(cumulative[-1][None, :] - cumulative) * step_size
    own_state = jnp.einsum("uh,uhp,un->hpn", to_end, inputs_f, in_float, precision=HIGHEST_PREC)
    own_log = cumulative[-1]
    group_logs, group_states = tuple(
        (
            part.astype(jnp.float32)
            for part in side_by_side(
                (own_log[None].astype(jnp.bfloat16), own_state[None].astype(jnp.bfloat16)),
                "grp",
                0,
                2,
            )
        )
    )
    group_index = jnp.arange(group_logs.shape[0])
    my_group = lax.axis_index("grp")
    inclusive = jnp.cumsum(group_logs, axis=0)
    exclusive = inclusive - group_logs
    before_me = jnp.sum(jnp.where((group_index == my_group)[:, None], exclusive, 0.0), axis=0)
    earlier_mask = (group_index < my_group)[:, None]
    weighting = jnp.where(
        earlier_mask, jnp.exp(jnp.where(earlier_mask, before_me[None, :] - inclusive, 0.0)), 0.0
    )
    entering = jnp.einsum("gh,ghpn->hpn", weighting, group_states, precision=HIGHEST_PREC)
    carried = jnp.exp(cumulative)[:, :, None] * jnp.einsum(
        "hpn,tn->thp", entering, out_float, precision=HIGHEST_PREC
    )
    ssm_out = inside + carried + skip_gain[None, :, None] * inputs_f
    gated_out = ssm_out.reshape(tok_rows, head_count * head_width) * jax.nn.silu(
        gate_input.astype(jnp.float32)
    )
    gated_gain = gated_out * norm_gain[None, :]
    squares = gated_out * gated_out
    proj_rows = lax.all_to_all(
        out_proj.reshape(dev_count, -1, out_proj.shape[1]), DEV, 0, 0, tiled=True
    )
    chan = proj_rows.shape[1]
    proj_rows = jnp.transpose(proj_rows, (1, 0, 2)).reshape(chan, model_dim)
    lane_pad = 128
    square_cols = (jnp.arange(lane_pad) == 0).astype(jnp.bfloat16)
    rhs = jnp.concatenate(
        [
            jnp.concatenate([proj_rows, jnp.zeros((chan, lane_pad), jnp.bfloat16)], axis=1),
            jnp.concatenate(
                [jnp.zeros((chan, model_dim), jnp.bfloat16), jnp.broadcast_to(square_cols, (chan, lane_pad))],
                axis=1,
            ),
        ],
        axis=0,
    )
    lhs = jnp.concatenate([gated_gain, squares], axis=1).astype(jnp.bfloat16)
    payload = jnp.dot(lhs, rhs, preferred_element_type=jnp.float32).astype(jnp.bfloat16)
    landed = lax.all_to_all(
        payload.reshape(dev_count, block_rows, payload.shape[1]), DEV, 0, 0, tiled=True
    )
    landed, expert_w = lax.optimization_barrier((landed, expert_w))
    landed = landed.astype(jnp.float32)
    summed_proj = jnp.sum(landed[:, :, :model_dim], axis=0)
    token_squares = jnp.sum(landed[:, :, model_dim], axis=0)
    mamba_out = (
        summed_proj * lax.rsqrt(token_squares / inner_dim + EPSILON)[:, None]
    ).astype(jnp.bfloat16)
    hidden_res = (residual.astype(jnp.float32) + mamba_out.astype(jnp.float32)).astype(jnp.bfloat16)
    hidden_float = hidden_res.astype(jnp.float32)
    normed = rms_scale(hidden_float, ffn_gain).astype(jnp.bfloat16)
    logits = jnp.dot(normed.astype(jnp.float32), router, precision=HIGHEST_PREC)
    expert_ids = jnp.arange(experts, dtype=jnp.int32)[None, :]
    first_logit = jnp.sum(logits * (routes[:, 0:1] == expert_ids).astype(jnp.float32), axis=1)
    second_logit = jnp.sum(logits * (routes[:, 1:2] == expert_ids).astype(jnp.float32), axis=1)
    first_prob = jax.nn.sigmoid(first_logit - second_logit)
    second_prob = 1.0 - first_prob
    placed = slot_tables(routes[None], experts, slot_cap)[0]
    filled = jnp.sum(placed, axis=1)
    outgoing = jnp.dot(
        filled.T.astype(jnp.bfloat16), normed, preferred_element_type=jnp.float32
    ).astype(jnp.bfloat16)
    outgoing = outgoing.reshape(experts, slot_cap, model_dim)
    arrived = lax.all_to_all(outgoing, "grp", split_axis=0, concat_axis=0, tiled=True)
    rows = lax.all_gather(arrived.reshape(-1, model_dim), "dev_1", axis=0, tiled=True)
    partial_down = 0.0
    for piece in expert_w:
        gate_act = jnp.dot(rows, piece[0], preferred_element_type=jnp.float32)
        up_act = jnp.dot(rows, piece[1], preferred_element_type=jnp.float32)
        hidden = (jax.nn.silu(gate_act) * up_act).astype(jnp.bfloat16)
        block_out = lax.dot_general(
            hidden, piece[2], (((1,), (1,)), ((), ())), preferred_element_type=jnp.float32
        ).astype(jnp.bfloat16)
        partial_down = partial_down + block_out.astype(jnp.float32)
    partial_down = partial_down.astype(jnp.bfloat16)
    summed = lax.psum_scatter(partial_down, "dev_1", scatter_dimension=0, tiled=True)
    returned = lax.all_to_all(
        summed.reshape(experts, slot_cap, model_dim), "grp", 0, 0, tiled=True
    ).astype(jnp.float32)
    weights = first_prob[:, None] * placed[:, 0, :] + second_prob[:, None] * placed[:, 1, :]
    contrib = jnp.dot(
        weights,
        returned.reshape(group_slots, model_dim),
        precision=HIGHEST_PREC,
    )
    return (hidden_float + contrib).astype(jnp.bfloat16)


def solution(mesh):
    torus = Mesh(mesh.devices.reshape(mesh.shape["grp"], 4, 8), ("grp", "dev_0", "dev_1"))
    in_specs = (
        P("grp", DEV),
        P("grp", DEV),
        P("grp", DEV),
        P(DEV),
        P("grp", None),
        P("grp", None),
        P(DEV),
        P(DEV),
        P(None, DEV),
        P(GRP_DEV, None),
        P(),
        P(),
        P(GRP_DEV, None),
        P("grp", None, DEV),
        P("grp", None, DEV),
        P("grp", DEV, None),
    )
    out_specs = P(GRP_DEV, None)
    return jax.shard_map(
        shards, mesh=torus, in_specs=in_specs, out_specs=out_specs, check_vma=False
    )
```

```python
import jax
import jax.numpy as jnp
from jax import lax
from jax.sharding import Mesh
from jax.sharding import PartitionSpec as P

DEV = ("dev_0", "dev_1")
GRP_DEV = ("grp", "dev_0", "dev_1")


EPSILON = 1e-05
HIGHEST_PREC = lax.Precision.HIGHEST


def side_by_side(arrays, axis, dim, along):
    columns = [a.reshape(*a.shape[:along], -1) for a in arrays]
    both = jnp.concatenate(columns, axis=along)
    filled, at, finished = (lax.all_gather(both, axis, axis=dim, tiled=True), 0, [])
    for a, column in zip(arrays, columns):
        piece = filled[..., at : at + column.shape[along]]
        finished.append(piece.reshape(*piece.shape[:along], *a.shape[along:]))
        at += column.shape[along]
    return tuple(finished)


def sent_to_all(shard, axis):
    peers = lax.axis_size(axis)
    return lax.all_to_all(
        jnp.broadcast_to(shard[None], (peers, *shard.shape)), axis, 0, 0, tiled=True
    )


def of_everyone(shard, axis):
    everything = sent_to_all(shard, axis)
    return jnp.sum(everything, axis=0)


def in_order(tiles, dim):
    dims = list(tiles.shape[1:])
    dims[dim] *= tiles.shape[0]
    return jnp.moveaxis(tiles, 0, dim).reshape(dims)


def collect(shard, axis, dim):
    return in_order(sent_to_all(shard, axis), dim)


def sum_by_axis(terms, axes):
    total = terms.astype(jnp.bfloat16)
    for axis in axes:
        total = lax.psum_scatter(total, axis, scatter_dimension=0, tiled=True)
    return total.astype(jnp.float32)


def ring_gather(shard, axis):
    size = lax.axis_size(axis)
    forward, backward, pieces = shard, shard, {0: shard}
    for step in range(1, size // 2 + 1):
        forward = lax.ppermute(forward, axis, [(i, (i + 1) % size) for i in range(size)])
        pieces[-step] = forward
        if step < size - step:
            backward = lax.ppermute(backward, axis, [(i, (i - 1) % size) for i in range(size)])
            pieces[step] = backward
    offsets = list(range(-(size // 2), size - size // 2))
    stacked = jnp.stack([pieces[o] for o in offsets])
    doubled = jnp.concatenate([stacked, stacked])
    start = (-offsets[0] - lax.axis_index(axis)) % size
    return lax.dynamic_slice_in_dim(doubled, start, size, 0)


def rms_scale(values, gain_vec):
    return (
        values * lax.rsqrt(jnp.mean(values * values, axis=-1, keepdims=True) + EPSILON) * gain_vec
    )


def slot_tables(routes_block, expert_count, slot_cap):
    blocks, row_total = (routes_block.shape[0], routes_block.shape[1])
    flat_routes = routes_block.reshape(blocks, row_total * 2)
    onehot = (
        flat_routes[:, :, None] == jnp.arange(expert_count, dtype=jnp.int32)[None, None, :]
    ).astype(jnp.int32)
    earlier = jnp.cumsum(onehot, axis=1) - onehot
    slot_rank = jnp.sum(earlier * onehot, axis=2)
    slot_index = (flat_routes * slot_cap + slot_rank).reshape(blocks, row_total, 2)
    placed = (
        slot_index[:, :, :, None]
        == jnp.arange(expert_count * slot_cap, dtype=jnp.int32)[None, None, None, :]
    )
    return placed.astype(jnp.float32)


def shards(
    ssm_input,
    gate_input,
    step_size,
    decay_rate,
    in_coeff,
    out_coeff,
    skip_gain,
    norm_gain,
    out_proj,
    residual,
    ffn_gain,
    router,
    routes,
    gate_weight,
    up_weight,
    down_weight,
):
    tok_rows = ssm_input.shape[0]
    head_count = step_size.shape[1]
    head_width = ssm_input.shape[1] // head_count
    dev_count = lax.axis_size(DEV)
    inner_dim = ssm_input.shape[1] * dev_count
    block_rows = residual.shape[0]
    model_dim = residual.shape[1]
    experts = lax.axis_size("grp")
    slot_cap = max(2, 4 * block_rows // experts)
    group_slots = experts * slot_cap
    inputs_f = ssm_input.astype(jnp.float32).reshape(tok_rows, head_count, head_width)
    in_float = in_coeff.astype(jnp.float32)
    out_float = out_coeff.astype(jnp.float32)
    log_rate = -(step_size * decay_rate[None, :])
    cumulative = jnp.cumsum(log_rate, axis=0)
    causal = (jnp.arange(tok_rows)[:, None] >= jnp.arange(tok_rows)[None, :])[:, :, None]
    spread = cumulative[:, None, :] - cumulative[None, :, :]
    decay_pair = jnp.where(causal, jnp.exp(jnp.where(causal, spread, 0.0)), 0.0)
    scores = jnp.dot(out_coeff, in_coeff.T, preferred_element_type=jnp.float32)
    mixing = decay_pair * scores[:, :, None] * step_size[None, :, :]
    inside = jnp.einsum("tuh,uhp->thp", mixing, inputs_f, precision=HIGHEST_PREC)
    to_end = jnp.exp(cumulative[-1][None, :] - cumulative) * step_size
    own_state = jnp.einsum("uh,uhp,un->hpn", to_end, inputs_f, in_float, precision=HIGHEST_PREC)
    own_log = cumulative[-1]
    group_logs, group_states = tuple(
        (
            part.astype(jnp.float32)
            for part in side_by_side(
                (own_log[None].astype(jnp.bfloat16), own_state[None].astype(jnp.bfloat16)),
                "grp",
                0,
                2,
            )
        )
    )
    group_index = jnp.arange(group_logs.shape[0])
    my_group = lax.axis_index("grp")
    inclusive = jnp.cumsum(group_logs, axis=0)
    exclusive = inclusive - group_logs
    before_me = jnp.sum(jnp.where((group_index == my_group)[:, None], exclusive, 0.0), axis=0)
    earlier_mask = (group_index < my_group)[:, None]
    weighting = jnp.where(
        earlier_mask, jnp.exp(jnp.where(earlier_mask, before_me[None, :] - inclusive, 0.0)), 0.0
    )
    entering = jnp.einsum("gh,ghpn->hpn", weighting, group_states, precision=HIGHEST_PREC)
    carried = jnp.exp(cumulative)[:, :, None] * jnp.einsum(
        "hpn,tn->thp", entering, out_float, precision=HIGHEST_PREC
    )
    ssm_out = inside + carried + skip_gain[None, :, None] * inputs_f
    gated_out = ssm_out.reshape(tok_rows, head_count * head_width) * jax.nn.silu(
        gate_input.astype(jnp.float32)
    )
    gated_gain = gated_out * norm_gain[None, :]
    squares = gated_out * gated_out
    proj_rows = lax.all_to_all(
        out_proj.reshape(dev_count, -1, out_proj.shape[1]), DEV, 0, 0, tiled=True
    )
    chan = proj_rows.shape[1]
    proj_rows = jnp.transpose(proj_rows, (1, 0, 2)).reshape(chan, model_dim)
    lane_pad = 128
    square_cols = (jnp.arange(lane_pad) == 0).astype(jnp.bfloat16)
    rhs = jnp.concatenate(
        [
            jnp.concatenate([proj_rows, jnp.zeros((chan, lane_pad), jnp.bfloat16)], axis=1),
            jnp.concatenate(
                [jnp.zeros((chan, model_dim), jnp.bfloat16), jnp.broadcast_to(square_cols, (chan, lane_pad))],
                axis=1,
            ),
        ],
        axis=0,
    )
    lhs = jnp.concatenate([gated_gain, squares], axis=1).astype(jnp.bfloat16)
    payload = jnp.dot(lhs, rhs, preferred_element_type=jnp.float32).astype(jnp.bfloat16)
    landed = lax.all_to_all(
        payload.reshape(dev_count, block_rows, payload.shape[1]), DEV, 0, 0, tiled=True
    ).astype(jnp.float32)
    summed_proj = jnp.sum(landed[:, :, :model_dim], axis=0)
    token_squares = jnp.sum(landed[:, :, model_dim], axis=0)
    mamba_out = (
        summed_proj * lax.rsqrt(token_squares / inner_dim + EPSILON)[:, None]
    ).astype(jnp.bfloat16)
    hidden_res = (residual.astype(jnp.float32) + mamba_out.astype(jnp.float32)).astype(jnp.bfloat16)
    hidden_float = hidden_res.astype(jnp.float32)
    normed = rms_scale(hidden_float, ffn_gain).astype(jnp.bfloat16)
    logits = jnp.dot(normed.astype(jnp.float32), router, precision=HIGHEST_PREC)
    expert_ids = jnp.arange(experts, dtype=jnp.int32)[None, :]
    first_logit = jnp.sum(logits * (routes[:, 0:1] == expert_ids).astype(jnp.float32), axis=1)
    second_logit = jnp.sum(logits * (routes[:, 1:2] == expert_ids).astype(jnp.float32), axis=1)
    first_prob = jax.nn.sigmoid(first_logit - second_logit)
    second_prob = 1.0 - first_prob
    placed = slot_tables(routes[None], experts, slot_cap)[0]
    filled = jnp.sum(placed, axis=1)
    outgoing = jnp.dot(
        filled.T.astype(jnp.bfloat16), normed, preferred_element_type=jnp.float32
    ).astype(jnp.bfloat16)
    outgoing = outgoing.reshape(experts, slot_cap, model_dim)
    arrived = lax.all_to_all(outgoing, "grp", split_axis=0, concat_axis=0, tiled=True)
    all_rows = arrived.reshape(-1, model_dim)
    all_rows = lax.all_gather(all_rows, "dev_0", axis=0, tiled=True)
    all_rows = lax.all_gather(all_rows, "dev_1", axis=0, tiled=True)
    hid_units = gate_weight.shape[2]
    both_act = jnp.dot(
        all_rows,
        jnp.concatenate([gate_weight[0], up_weight[0]], axis=1),
        preferred_element_type=jnp.float32,
    )
    hidden = (jax.nn.silu(both_act[:, :hid_units]) * both_act[:, hid_units:]).astype(jnp.bfloat16)
    hidden = lax.optimization_barrier(hidden)
    partial_down = jnp.dot(hidden, down_weight[0], preferred_element_type=jnp.float32)
    summed = lax.psum_scatter(
        partial_down.astype(jnp.bfloat16), "dev_1", scatter_dimension=0, tiled=True
    )
    x_count = lax.axis_size("dev_0")
    summed = jnp.swapaxes(summed.reshape(x_count, experts, slot_cap, model_dim), 0, 1)
    landed_back = lax.all_to_all(
        summed.reshape(experts * x_count, slot_cap, model_dim), ("grp", "dev_0"), 0, 0, tiled=True
    )
    returned = jnp.sum(
        landed_back.reshape(experts, x_count, slot_cap, model_dim).astype(jnp.float32), axis=1
    )
    weights = first_prob[:, None] * placed[:, 0, :] + second_prob[:, None] * placed[:, 1, :]
    contrib = jnp.dot(
        weights,
        returned.reshape(group_slots, model_dim),
        precision=HIGHEST_PREC,
    )
    return (hidden_float + contrib).astype(jnp.bfloat16)


def solution(mesh):
    torus = Mesh(mesh.devices.reshape(mesh.shape["grp"], 4, 8), ("grp", "dev_0", "dev_1"))
    in_specs = (
        P("grp", DEV),
        P("grp", DEV),
        P("grp", DEV),
        P(DEV),
        P("grp", None),
        P("grp", None),
        P(DEV),
        P(DEV),
        P(None, DEV),
        P(GRP_DEV, None),
        P(),
        P(),
        P(GRP_DEV, None),
        P("grp", None, DEV),
        P("grp", None, DEV),
        P("grp", DEV, None),
    )
    out_specs = P(GRP_DEV, None)
    return jax.shard_map(
        shards, mesh=torus, in_specs=in_specs, out_specs=out_specs, check_vma=False
    )
```

```python
import jax
import jax.numpy as jnp
from jax import lax
from jax.sharding import Mesh
from jax.sharding import PartitionSpec as P

DEV = ("dev_0", "dev_1")
GRP_DEV = ("grp", "dev_0", "dev_1")


EPSILON = 1e-05
HIGHEST_PREC = lax.Precision.HIGHEST


def side_by_side(arrays, axis, dim, along):
    columns = [a.reshape(*a.shape[:along], -1) for a in arrays]
    both = jnp.concatenate(columns, axis=along)
    filled, at, finished = (lax.all_gather(both, axis, axis=dim, tiled=True), 0, [])
    for a, column in zip(arrays, columns):
        piece = filled[..., at : at + column.shape[along]]
        finished.append(piece.reshape(*piece.shape[:along], *a.shape[along:]))
        at += column.shape[along]
    return tuple(finished)


def sent_to_all(shard, axis):
    peers = lax.axis_size(axis)
    return lax.all_to_all(
        jnp.broadcast_to(shard[None], (peers, *shard.shape)), axis, 0, 0, tiled=True
    )


def of_everyone(shard, axis):
    everything = sent_to_all(shard, axis)
    return jnp.sum(everything, axis=0)


def in_order(tiles, dim):
    dims = list(tiles.shape[1:])
    dims[dim] *= tiles.shape[0]
    return jnp.moveaxis(tiles, 0, dim).reshape(dims)


def collect(shard, axis, dim):
    return in_order(sent_to_all(shard, axis), dim)


def sum_by_axis(terms, axes):
    total = terms.astype(jnp.bfloat16)
    for axis in axes:
        total = lax.psum_scatter(total, axis, scatter_dimension=0, tiled=True)
    return total.astype(jnp.float32)


def ring_gather(shard, axis):
    size = lax.axis_size(axis)
    forward, backward, pieces = shard, shard, {0: shard}
    for step in range(1, size // 2 + 1):
        forward = lax.ppermute(forward, axis, [(i, (i + 1) % size) for i in range(size)])
        pieces[-step] = forward
        if step < size - step:
            backward = lax.ppermute(backward, axis, [(i, (i - 1) % size) for i in range(size)])
            pieces[step] = backward
    offsets = list(range(-(size // 2), size - size // 2))
    stacked = jnp.stack([pieces[o] for o in offsets])
    doubled = jnp.concatenate([stacked, stacked])
    start = (-offsets[0] - lax.axis_index(axis)) % size
    return lax.dynamic_slice_in_dim(doubled, start, size, 0)


def rms_scale(values, gain_vec):
    return (
        values * lax.rsqrt(jnp.mean(values * values, axis=-1, keepdims=True) + EPSILON) * gain_vec
    )


def slot_tables(routes_block, expert_count, slot_cap):
    blocks, row_total = (routes_block.shape[0], routes_block.shape[1])
    flat_routes = routes_block.reshape(blocks, row_total * 2)
    onehot = (
        flat_routes[:, :, None] == jnp.arange(expert_count, dtype=jnp.int32)[None, None, :]
    ).astype(jnp.int32)
    earlier = jnp.cumsum(onehot, axis=1) - onehot
    slot_rank = jnp.sum(earlier * onehot, axis=2)
    slot_index = (flat_routes * slot_cap + slot_rank).reshape(blocks, row_total, 2)
    placed = (
        slot_index[:, :, :, None]
        == jnp.arange(expert_count * slot_cap, dtype=jnp.int32)[None, None, None, :]
    )
    return placed.astype(jnp.float32)


def shards(
    ssm_input,
    gate_input,
    step_size,
    decay_rate,
    in_coeff,
    out_coeff,
    skip_gain,
    norm_gain,
    out_proj,
    residual,
    ffn_gain,
    router,
    routes,
    gate_weight,
    up_weight,
    down_weight,
):
    tok_rows = ssm_input.shape[0]
    head_count = step_size.shape[1]
    head_width = ssm_input.shape[1] // head_count
    dev_count = lax.axis_size(DEV)
    inner_dim = ssm_input.shape[1] * dev_count
    block_rows = residual.shape[0]
    model_dim = residual.shape[1]
    experts = lax.axis_size("grp")
    slot_cap = max(2, 4 * block_rows // experts)
    group_slots = experts * slot_cap
    inputs_f = ssm_input.astype(jnp.float32).reshape(tok_rows, head_count, head_width)
    in_float = in_coeff.astype(jnp.float32)
    out_float = out_coeff.astype(jnp.float32)
    log_rate = -(step_size * decay_rate[None, :])
    cumulative = jnp.cumsum(log_rate, axis=0)
    causal = (jnp.arange(tok_rows)[:, None] >= jnp.arange(tok_rows)[None, :])[:, :, None]
    spread = cumulative[:, None, :] - cumulative[None, :, :]
    decay_pair = jnp.where(causal, jnp.exp(jnp.where(causal, spread, 0.0)), 0.0)
    scores = jnp.dot(out_coeff, in_coeff.T, preferred_element_type=jnp.float32)
    mixing = decay_pair * scores[:, :, None] * step_size[None, :, :]
    inside = jnp.einsum("tuh,uhp->thp", mixing, inputs_f, precision=HIGHEST_PREC)
    to_end = jnp.exp(cumulative[-1][None, :] - cumulative) * step_size
    own_state = jnp.einsum("uh,uhp,un->hpn", to_end, inputs_f, in_float, precision=HIGHEST_PREC)
    own_log = cumulative[-1]
    group_logs, group_states = tuple(
        (
            part.astype(jnp.float32)
            for part in side_by_side(
                (own_log[None].astype(jnp.bfloat16), own_state[None].astype(jnp.bfloat16)),
                "grp",
                0,
                2,
            )
        )
    )
    group_index = jnp.arange(group_logs.shape[0])
    my_group = lax.axis_index("grp")
    inclusive = jnp.cumsum(group_logs, axis=0)
    exclusive = inclusive - group_logs
    before_me = jnp.sum(jnp.where((group_index == my_group)[:, None], exclusive, 0.0), axis=0)
    earlier_mask = (group_index < my_group)[:, None]
    weighting = jnp.where(
        earlier_mask, jnp.exp(jnp.where(earlier_mask, before_me[None, :] - inclusive, 0.0)), 0.0
    )
    entering = jnp.einsum("gh,ghpn->hpn", weighting, group_states, precision=HIGHEST_PREC)
    carried = jnp.exp(cumulative)[:, :, None] * jnp.einsum(
        "hpn,tn->thp", entering, out_float, precision=HIGHEST_PREC
    )
    ssm_out = inside + carried + skip_gain[None, :, None] * inputs_f
    gated_out = ssm_out.reshape(tok_rows, head_count * head_width) * jax.nn.silu(
        gate_input.astype(jnp.float32)
    )
    gated_gain = gated_out * norm_gain[None, :]
    squares = gated_out * gated_out
    proj_rows = lax.all_to_all(
        out_proj.reshape(dev_count, -1, out_proj.shape[1]), DEV, 0, 0, tiled=True
    )
    chan = proj_rows.shape[1]
    proj_rows = jnp.transpose(proj_rows, (1, 0, 2)).reshape(chan, model_dim)
    lane_pad = 128
    square_cols = (jnp.arange(lane_pad) == 0).astype(jnp.bfloat16)
    rhs = jnp.concatenate(
        [
            jnp.concatenate([proj_rows, jnp.zeros((chan, lane_pad), jnp.bfloat16)], axis=1),
            jnp.concatenate(
                [jnp.zeros((chan, model_dim), jnp.bfloat16), jnp.broadcast_to(square_cols, (chan, lane_pad))],
                axis=1,
            ),
        ],
        axis=0,
    )
    lhs = jnp.concatenate([gated_gain, squares], axis=1).astype(jnp.bfloat16)
    payload = jnp.dot(lhs, rhs, preferred_element_type=jnp.float32).astype(jnp.bfloat16)
    landed = lax.all_to_all(
        payload.reshape(dev_count, block_rows, payload.shape[1]), DEV, 0, 0, tiled=True
    ).astype(jnp.float32)
    summed_proj = jnp.sum(landed[:, :, :model_dim], axis=0)
    token_squares = jnp.sum(landed[:, :, model_dim], axis=0)
    mamba_out = (
        summed_proj * lax.rsqrt(token_squares / inner_dim + EPSILON)[:, None]
    ).astype(jnp.bfloat16)
    hidden_res = (residual.astype(jnp.float32) + mamba_out.astype(jnp.float32)).astype(jnp.bfloat16)
    hidden_float = hidden_res.astype(jnp.float32)
    normed = rms_scale(hidden_float, ffn_gain).astype(jnp.bfloat16)
    logits = jnp.dot(normed.astype(jnp.float32), router, precision=HIGHEST_PREC)
    expert_ids = jnp.arange(experts, dtype=jnp.int32)[None, :]
    first_logit = jnp.sum(logits * (routes[:, 0:1] == expert_ids).astype(jnp.float32), axis=1)
    second_logit = jnp.sum(logits * (routes[:, 1:2] == expert_ids).astype(jnp.float32), axis=1)
    first_prob = jax.nn.sigmoid(first_logit - second_logit)
    second_prob = 1.0 - first_prob
    placed = slot_tables(routes[None], experts, slot_cap)[0]
    filled = jnp.sum(placed, axis=1)
    outgoing = jnp.dot(
        filled.T.astype(jnp.bfloat16), normed, preferred_element_type=jnp.float32
    ).astype(jnp.bfloat16)
    outgoing = outgoing.reshape(experts, slot_cap, model_dim)
    x_count = lax.axis_size("dev_0")
    outgoing = jnp.broadcast_to(outgoing[:, None], (experts, x_count, slot_cap, model_dim))
    arrived = lax.all_to_all(
        outgoing.reshape(experts * x_count, slot_cap, model_dim), ("grp", "dev_0"), 0, 0, tiled=True
    )
    all_rows = lax.all_gather(arrived.reshape(-1, model_dim), "dev_1", axis=0, tiled=True)
    hid_units = gate_weight.shape[2]
    both_act = jnp.dot(
        all_rows,
        jnp.concatenate([gate_weight[0], up_weight[0]], axis=1),
        preferred_element_type=jnp.float32,
    )
    hidden = (jax.nn.silu(both_act[:, :hid_units]) * both_act[:, hid_units:]).astype(jnp.bfloat16)
    hidden = lax.optimization_barrier(hidden)
    partial_down = jnp.dot(hidden, down_weight[0], preferred_element_type=jnp.float32)
    summed = lax.psum_scatter(
        partial_down.astype(jnp.bfloat16), "dev_1", scatter_dimension=0, tiled=True
    )
    landed_back = lax.all_to_all(
        summed.reshape(experts * x_count, slot_cap, model_dim), ("grp", "dev_0"), 0, 0, tiled=True
    )
    returned = jnp.sum(
        landed_back.reshape(experts, x_count, slot_cap, model_dim).astype(jnp.float32), axis=1
    )
    weights = first_prob[:, None] * placed[:, 0, :] + second_prob[:, None] * placed[:, 1, :]
    contrib = jnp.dot(
        weights,
        returned.reshape(group_slots, model_dim),
        precision=HIGHEST_PREC,
    )
    return (hidden_float + contrib).astype(jnp.bfloat16)


def solution(mesh):
    torus = Mesh(mesh.devices.reshape(mesh.shape["grp"], 4, 8), ("grp", "dev_0", "dev_1"))
    in_specs = (
        P("grp", DEV),
        P("grp", DEV),
        P("grp", DEV),
        P(DEV),
        P("grp", None),
        P("grp", None),
        P(DEV),
        P(DEV),
        P(None, DEV),
        P(GRP_DEV, None),
        P(),
        P(),
        P(GRP_DEV, None),
        P("grp", None, DEV),
        P("grp", None, DEV),
        P("grp", DEV, None),
    )
    out_specs = P(GRP_DEV, None)
    return jax.shard_map(
        shards, mesh=torus, in_specs=in_specs, out_specs=out_specs, check_vma=False
    )
```

```python
import jax
import jax.numpy as jnp
from jax import lax
from jax.sharding import Mesh
from jax.sharding import PartitionSpec as P

DEV = ("dev_0", "dev_1")
GRP_DEV = ("grp", "dev_0", "dev_1")


EPSILON = 1e-05
HIGHEST_PREC = lax.Precision.HIGHEST


def side_by_side(arrays, axis, dim, along):
    columns = [a.reshape(*a.shape[:along], -1) for a in arrays]
    both = jnp.concatenate(columns, axis=along)
    filled, at, finished = (lax.all_gather(both, axis, axis=dim, tiled=True), 0, [])
    for a, column in zip(arrays, columns):
        piece = filled[..., at : at + column.shape[along]]
        finished.append(piece.reshape(*piece.shape[:along], *a.shape[along:]))
        at += column.shape[along]
    return tuple(finished)


def sent_to_all(shard, axis):
    peers = lax.axis_size(axis)
    return lax.all_to_all(
        jnp.broadcast_to(shard[None], (peers, *shard.shape)), axis, 0, 0, tiled=True
    )


def of_everyone(shard, axis):
    everything = sent_to_all(shard, axis)
    return jnp.sum(everything, axis=0)


def in_order(tiles, dim):
    dims = list(tiles.shape[1:])
    dims[dim] *= tiles.shape[0]
    return jnp.moveaxis(tiles, 0, dim).reshape(dims)


def collect(shard, axis, dim):
    return in_order(sent_to_all(shard, axis), dim)


def sum_by_axis(terms, axes):
    total = terms.astype(jnp.bfloat16)
    for axis in axes:
        total = lax.psum_scatter(total, axis, scatter_dimension=0, tiled=True)
    return total.astype(jnp.float32)


def ring_gather(shard, axis):
    size = lax.axis_size(axis)
    forward, backward, pieces = shard, shard, {0: shard}
    for step in range(1, size // 2 + 1):
        forward = lax.ppermute(forward, axis, [(i, (i + 1) % size) for i in range(size)])
        pieces[-step] = forward
        if step < size - step:
            backward = lax.ppermute(backward, axis, [(i, (i - 1) % size) for i in range(size)])
            pieces[step] = backward
    offsets = list(range(-(size // 2), size - size // 2))
    stacked = jnp.stack([pieces[o] for o in offsets])
    doubled = jnp.concatenate([stacked, stacked])
    start = (-offsets[0] - lax.axis_index(axis)) % size
    return lax.dynamic_slice_in_dim(doubled, start, size, 0)


def rms_scale(values, gain_vec):
    return (
        values * lax.rsqrt(jnp.mean(values * values, axis=-1, keepdims=True) + EPSILON) * gain_vec
    )


def slot_tables(routes_block, expert_count, slot_cap):
    blocks, row_total = (routes_block.shape[0], routes_block.shape[1])
    flat_routes = routes_block.reshape(blocks, row_total * 2)
    onehot = (
        flat_routes[:, :, None] == jnp.arange(expert_count, dtype=jnp.int32)[None, None, :]
    ).astype(jnp.int32)
    earlier = jnp.cumsum(onehot, axis=1) - onehot
    slot_rank = jnp.sum(earlier * onehot, axis=2)
    slot_index = (flat_routes * slot_cap + slot_rank).reshape(blocks, row_total, 2)
    placed = (
        slot_index[:, :, :, None]
        == jnp.arange(expert_count * slot_cap, dtype=jnp.int32)[None, None, None, :]
    )
    return placed.astype(jnp.float32)


def shards(
    ssm_input,
    gate_input,
    step_size,
    decay_rate,
    in_coeff,
    out_coeff,
    skip_gain,
    norm_gain,
    out_proj,
    residual,
    ffn_gain,
    router,
    routes,
    gate_weight,
    up_weight,
    down_weight,
):
    tok_rows = ssm_input.shape[0]
    head_count = step_size.shape[1]
    head_width = ssm_input.shape[1] // head_count
    dev_count = lax.axis_size(DEV)
    inner_dim = ssm_input.shape[1] * dev_count
    block_rows = residual.shape[0]
    model_dim = residual.shape[1]
    experts = lax.axis_size("grp")
    slot_cap = max(2, 4 * block_rows // experts)
    group_slots = experts * slot_cap
    inputs_f = ssm_input.astype(jnp.float32).reshape(tok_rows, head_count, head_width)
    in_float = in_coeff.astype(jnp.float32)
    out_float = out_coeff.astype(jnp.float32)
    log_rate = -(step_size * decay_rate[None, :])
    cumulative = jnp.cumsum(log_rate, axis=0)
    causal = (jnp.arange(tok_rows)[:, None] >= jnp.arange(tok_rows)[None, :])[:, :, None]
    spread = cumulative[:, None, :] - cumulative[None, :, :]
    decay_pair = jnp.where(causal, jnp.exp(jnp.where(causal, spread, 0.0)), 0.0)
    scores = jnp.dot(out_coeff, in_coeff.T, preferred_element_type=jnp.float32)
    mixing = decay_pair * scores[:, :, None] * step_size[None, :, :]
    inside = jnp.einsum("tuh,uhp->thp", mixing, inputs_f, precision=HIGHEST_PREC)
    to_end = jnp.exp(cumulative[-1][None, :] - cumulative) * step_size
    own_state = jnp.einsum("uh,uhp,un->hpn", to_end, inputs_f, in_float, precision=HIGHEST_PREC)
    own_log = cumulative[-1]
    group_logs, group_states = tuple(
        (
            part.astype(jnp.float32)
            for part in side_by_side(
                (own_log[None].astype(jnp.bfloat16), own_state[None].astype(jnp.bfloat16)),
                "grp",
                0,
                2,
            )
        )
    )
    group_index = jnp.arange(group_logs.shape[0])
    my_group = lax.axis_index("grp")
    inclusive = jnp.cumsum(group_logs, axis=0)
    exclusive = inclusive - group_logs
    before_me = jnp.sum(jnp.where((group_index == my_group)[:, None], exclusive, 0.0), axis=0)
    earlier_mask = (group_index < my_group)[:, None]
    weighting = jnp.where(
        earlier_mask, jnp.exp(jnp.where(earlier_mask, before_me[None, :] - inclusive, 0.0)), 0.0
    )
    entering = jnp.einsum("gh,ghpn->hpn", weighting, group_states, precision=HIGHEST_PREC)
    carried = jnp.exp(cumulative)[:, :, None] * jnp.einsum(
        "hpn,tn->thp", entering, out_float, precision=HIGHEST_PREC
    )
    ssm_out = inside + carried + skip_gain[None, :, None] * inputs_f
    gated_out = ssm_out.reshape(tok_rows, head_count * head_width) * jax.nn.silu(
        gate_input.astype(jnp.float32)
    )
    gated_gain = gated_out * norm_gain[None, :]
    squares = gated_out * gated_out
    proj_rows = lax.all_to_all(
        out_proj.reshape(dev_count, -1, out_proj.shape[1]), DEV, 0, 0, tiled=True
    )
    chan = proj_rows.shape[1]
    proj_rows = jnp.transpose(proj_rows, (1, 0, 2)).reshape(chan, model_dim)
    lane_pad = 128
    square_cols = (jnp.arange(lane_pad) == 0).astype(jnp.bfloat16)
    rhs = jnp.concatenate(
        [
            jnp.concatenate([proj_rows, jnp.zeros((chan, lane_pad), jnp.bfloat16)], axis=1),
            jnp.concatenate(
                [jnp.zeros((chan, model_dim), jnp.bfloat16), jnp.broadcast_to(square_cols, (chan, lane_pad))],
                axis=1,
            ),
        ],
        axis=0,
    )
    lhs = jnp.concatenate([gated_gain, squares], axis=1).astype(jnp.bfloat16)
    payload = jnp.dot(lhs, rhs, preferred_element_type=jnp.float32).astype(jnp.bfloat16)
    x_count = lax.axis_size("dev_0")
    y_count = lax.axis_size("dev_1")
    by_x = lax.all_to_all(
        payload.reshape(x_count, y_count, block_rows, payload.shape[1]), "dev_0", 0, 0, tiled=True
    )
    by_x = jnp.sum(by_x.astype(jnp.float32), axis=0).astype(jnp.bfloat16)
    landed = lax.all_to_all(by_x, "dev_1", 0, 0, tiled=True)
    landed = jnp.sum(landed.astype(jnp.float32), axis=0)
    summed_proj = landed[:, :model_dim]
    token_squares = landed[:, model_dim]
    mamba_out = (
        summed_proj * lax.rsqrt(token_squares / inner_dim + EPSILON)[:, None]
    ).astype(jnp.bfloat16)
    hidden_res = (residual.astype(jnp.float32) + mamba_out.astype(jnp.float32)).astype(jnp.bfloat16)
    hidden_float = hidden_res.astype(jnp.float32)
    normed = rms_scale(hidden_float, ffn_gain).astype(jnp.bfloat16)
    logits = jnp.dot(normed.astype(jnp.float32), router, precision=HIGHEST_PREC)
    expert_ids = jnp.arange(experts, dtype=jnp.int32)[None, :]
    first_logit = jnp.sum(logits * (routes[:, 0:1] == expert_ids).astype(jnp.float32), axis=1)
    second_logit = jnp.sum(logits * (routes[:, 1:2] == expert_ids).astype(jnp.float32), axis=1)
    first_prob = jax.nn.sigmoid(first_logit - second_logit)
    second_prob = 1.0 - first_prob
    placed = slot_tables(routes[None], experts, slot_cap)[0]
    filled = jnp.sum(placed, axis=1)
    outgoing = jnp.dot(
        filled.T.astype(jnp.bfloat16), normed, preferred_element_type=jnp.float32
    ).astype(jnp.bfloat16)
    outgoing = outgoing.reshape(experts, slot_cap, model_dim)
    outgoing = jnp.broadcast_to(outgoing[:, None], (experts, x_count, slot_cap, model_dim))
    arrived = lax.all_to_all(
        outgoing.reshape(experts * x_count, slot_cap, model_dim), ("grp", "dev_0"), 0, 0, tiled=True
    )
    all_rows = lax.all_gather(arrived.reshape(-1, model_dim), "dev_1", axis=0, tiled=True)
    hid_units = gate_weight.shape[2]
    both_act = jnp.dot(
        all_rows,
        jnp.concatenate([gate_weight[0], up_weight[0]], axis=1),
        preferred_element_type=jnp.float32,
    )
    hidden = (jax.nn.silu(both_act[:, :hid_units]) * both_act[:, hid_units:]).astype(jnp.bfloat16)
    hidden = lax.optimization_barrier(hidden)
    partial_down = jnp.dot(hidden, down_weight[0], preferred_element_type=jnp.float32)
    summed = lax.psum_scatter(
        partial_down.astype(jnp.bfloat16), "dev_1", scatter_dimension=0, tiled=True
    )
    landed_back = lax.all_to_all(
        summed.reshape(experts * x_count, slot_cap, model_dim), ("grp", "dev_0"), 0, 0, tiled=True
    )
    returned = jnp.sum(
        landed_back.reshape(experts, x_count, slot_cap, model_dim).astype(jnp.float32), axis=1
    )
    weights = first_prob[:, None] * placed[:, 0, :] + second_prob[:, None] * placed[:, 1, :]
    contrib = jnp.dot(
        weights,
        returned.reshape(group_slots, model_dim),
        precision=HIGHEST_PREC,
    )
    return (hidden_float + contrib).astype(jnp.bfloat16)


def solution(mesh):
    torus = Mesh(mesh.devices.reshape(mesh.shape["grp"], 4, 8), ("grp", "dev_0", "dev_1"))
    in_specs = (
        P("grp", DEV),
        P("grp", DEV),
        P("grp", DEV),
        P(DEV),
        P("grp", None),
        P("grp", None),
        P(DEV),
        P(DEV),
        P(None, DEV),
        P(GRP_DEV, None),
        P(),
        P(),
        P(GRP_DEV, None),
        P("grp", None, DEV),
        P("grp", None, DEV),
        P("grp", DEV, None),
    )
    out_specs = P(GRP_DEV, None)
    return jax.shard_map(
        shards, mesh=torus, in_specs=in_specs, out_specs=out_specs, check_vma=False
    )
```

```python
import jax
import jax.numpy as jnp
from jax import lax
from jax.sharding import Mesh
from jax.sharding import PartitionSpec as P

DEV = ("dev_0", "dev_1")
GRP_DEV = ("grp", "dev_0", "dev_1")


EPSILON = 1e-05
HIGHEST_PREC = lax.Precision.HIGHEST


def side_by_side(arrays, axis, dim, along):
    columns = [a.reshape(*a.shape[:along], -1) for a in arrays]
    both = jnp.concatenate(columns, axis=along)
    filled, at, finished = (lax.all_gather(both, axis, axis=dim, tiled=True), 0, [])
    for a, column in zip(arrays, columns):
        piece = filled[..., at : at + column.shape[along]]
        finished.append(piece.reshape(*piece.shape[:along], *a.shape[along:]))
        at += column.shape[along]
    return tuple(finished)


def sent_to_all(shard, axis):
    peers = lax.axis_size(axis)
    return lax.all_to_all(
        jnp.broadcast_to(shard[None], (peers, *shard.shape)), axis, 0, 0, tiled=True
    )


def of_everyone(shard, axis):
    everything = sent_to_all(shard, axis)
    return jnp.sum(everything, axis=0)


def in_order(tiles, dim):
    dims = list(tiles.shape[1:])
    dims[dim] *= tiles.shape[0]
    return jnp.moveaxis(tiles, 0, dim).reshape(dims)


def collect(shard, axis, dim):
    return in_order(sent_to_all(shard, axis), dim)


def sum_by_axis(terms, axes):
    total = terms.astype(jnp.bfloat16)
    for axis in axes:
        total = lax.psum_scatter(total, axis, scatter_dimension=0, tiled=True)
    return total.astype(jnp.float32)


def ring_gather(shard, axis):
    size = lax.axis_size(axis)
    forward, backward, pieces = shard, shard, {0: shard}
    for step in range(1, size // 2 + 1):
        forward = lax.ppermute(forward, axis, [(i, (i + 1) % size) for i in range(size)])
        pieces[-step] = forward
        if step < size - step:
            backward = lax.ppermute(backward, axis, [(i, (i - 1) % size) for i in range(size)])
            pieces[step] = backward
    offsets = list(range(-(size // 2), size - size // 2))
    stacked = jnp.stack([pieces[o] for o in offsets])
    doubled = jnp.concatenate([stacked, stacked])
    start = (-offsets[0] - lax.axis_index(axis)) % size
    return lax.dynamic_slice_in_dim(doubled, start, size, 0)


def rms_scale(values, gain_vec):
    return (
        values * lax.rsqrt(jnp.mean(values * values, axis=-1, keepdims=True) + EPSILON) * gain_vec
    )


def slot_tables(routes_block, expert_count, slot_cap):
    blocks, row_total = (routes_block.shape[0], routes_block.shape[1])
    flat_routes = routes_block.reshape(blocks, row_total * 2)
    onehot = (
        flat_routes[:, :, None] == jnp.arange(expert_count, dtype=jnp.int32)[None, None, :]
    ).astype(jnp.int32)
    earlier = jnp.cumsum(onehot, axis=1) - onehot
    slot_rank = jnp.sum(earlier * onehot, axis=2)
    slot_index = (flat_routes * slot_cap + slot_rank).reshape(blocks, row_total, 2)
    placed = (
        slot_index[:, :, :, None]
        == jnp.arange(expert_count * slot_cap, dtype=jnp.int32)[None, None, None, :]
    )
    return placed.astype(jnp.float32)


def shards(
    ssm_input,
    gate_input,
    step_size,
    decay_rate,
    in_coeff,
    out_coeff,
    skip_gain,
    norm_gain,
    out_proj,
    residual,
    ffn_gain,
    router,
    routes,
    gate_weight,
    up_weight,
    down_weight,
):
    tok_rows = ssm_input.shape[0]
    head_count = step_size.shape[1]
    head_width = ssm_input.shape[1] // head_count
    dev_count = lax.axis_size(DEV)
    inner_dim = ssm_input.shape[1] * dev_count
    block_rows = residual.shape[0]
    model_dim = residual.shape[1]
    experts = lax.axis_size("grp")
    slot_cap = max(2, 4 * block_rows // experts)
    group_slots = experts * slot_cap
    inputs_f = ssm_input.astype(jnp.float32).reshape(tok_rows, head_count, head_width)
    in_float = in_coeff.astype(jnp.float32)
    out_float = out_coeff.astype(jnp.float32)
    log_rate = -(step_size * decay_rate[None, :])
    cumulative = jnp.cumsum(log_rate, axis=0)
    causal = (jnp.arange(tok_rows)[:, None] >= jnp.arange(tok_rows)[None, :])[:, :, None]
    spread = cumulative[:, None, :] - cumulative[None, :, :]
    decay_pair = jnp.where(causal, jnp.exp(jnp.where(causal, spread, 0.0)), 0.0)
    scores = jnp.dot(out_coeff, in_coeff.T, preferred_element_type=jnp.float32)
    mixing = decay_pair * scores[:, :, None] * step_size[None, :, :]
    inside = jnp.einsum("tuh,uhp->thp", mixing, inputs_f, precision=HIGHEST_PREC)
    to_end = jnp.exp(cumulative[-1][None, :] - cumulative) * step_size
    own_state = jnp.einsum("uh,uhp,un->hpn", to_end, inputs_f, in_float, precision=HIGHEST_PREC)
    own_log = cumulative[-1]
    group_logs, group_states = tuple(
        (
            part.astype(jnp.float32)
            for part in side_by_side(
                (own_log[None].astype(jnp.bfloat16), own_state[None].astype(jnp.bfloat16)),
                "grp",
                0,
                2,
            )
        )
    )
    group_index = jnp.arange(group_logs.shape[0])
    my_group = lax.axis_index("grp")
    inclusive = jnp.cumsum(group_logs, axis=0)
    exclusive = inclusive - group_logs
    before_me = jnp.sum(jnp.where((group_index == my_group)[:, None], exclusive, 0.0), axis=0)
    earlier_mask = (group_index < my_group)[:, None]
    weighting = jnp.where(
        earlier_mask, jnp.exp(jnp.where(earlier_mask, before_me[None, :] - inclusive, 0.0)), 0.0
    )
    entering = jnp.einsum("gh,ghpn->hpn", weighting, group_states, precision=HIGHEST_PREC)
    carried = jnp.exp(cumulative)[:, :, None] * jnp.einsum(
        "hpn,tn->thp", entering, out_float, precision=HIGHEST_PREC
    )
    ssm_out = inside + carried + skip_gain[None, :, None] * inputs_f
    gated_out = ssm_out.reshape(tok_rows, head_count * head_width) * jax.nn.silu(
        gate_input.astype(jnp.float32)
    )
    gated_gain = gated_out * norm_gain[None, :]
    squares = gated_out * gated_out
    proj_rows = lax.all_to_all(
        out_proj.reshape(dev_count, -1, out_proj.shape[1]), DEV, 0, 0, tiled=True
    )
    chan = proj_rows.shape[1]
    proj_rows = jnp.transpose(proj_rows, (1, 0, 2)).reshape(chan, model_dim)
    lane_pad = 128
    square_cols = (jnp.arange(lane_pad) == 0).astype(jnp.bfloat16)
    rhs = jnp.concatenate(
        [
            jnp.concatenate([proj_rows, jnp.zeros((chan, lane_pad), jnp.bfloat16)], axis=1),
            jnp.concatenate(
                [jnp.zeros((chan, model_dim), jnp.bfloat16), jnp.broadcast_to(square_cols, (chan, lane_pad))],
                axis=1,
            ),
        ],
        axis=0,
    )
    lhs = jnp.concatenate([gated_gain, squares], axis=1).astype(jnp.bfloat16)
    payload = jnp.dot(lhs, rhs, preferred_element_type=jnp.float32).astype(jnp.bfloat16)
    x_count = lax.axis_size("dev_0")
    y_count = lax.axis_size("dev_1")
    by_y = lax.all_to_all(
        jnp.swapaxes(payload.reshape(x_count, y_count, block_rows, payload.shape[1]), 0, 1),
        "dev_1",
        0,
        0,
        tiled=True,
    )
    by_y = jnp.sum(by_y.astype(jnp.float32), axis=0).astype(jnp.bfloat16)
    landed = lax.all_to_all(by_y, "dev_0", 0, 0, tiled=True)
    landed = jnp.sum(landed.astype(jnp.float32), axis=0)
    summed_proj = landed[:, :model_dim]
    token_squares = landed[:, model_dim]
    mamba_out = (
        summed_proj * lax.rsqrt(token_squares / inner_dim + EPSILON)[:, None]
    ).astype(jnp.bfloat16)
    hidden_res = (residual.astype(jnp.float32) + mamba_out.astype(jnp.float32)).astype(jnp.bfloat16)
    hidden_float = hidden_res.astype(jnp.float32)
    normed = rms_scale(hidden_float, ffn_gain).astype(jnp.bfloat16)
    logits = jnp.dot(normed.astype(jnp.float32), router, precision=HIGHEST_PREC)
    expert_ids = jnp.arange(experts, dtype=jnp.int32)[None, :]
    first_logit = jnp.sum(logits * (routes[:, 0:1] == expert_ids).astype(jnp.float32), axis=1)
    second_logit = jnp.sum(logits * (routes[:, 1:2] == expert_ids).astype(jnp.float32), axis=1)
    first_prob = jax.nn.sigmoid(first_logit - second_logit)
    second_prob = 1.0 - first_prob
    placed = slot_tables(routes[None], experts, slot_cap)[0]
    filled = jnp.sum(placed, axis=1)
    outgoing = jnp.dot(
        filled.T.astype(jnp.bfloat16), normed, preferred_element_type=jnp.float32
    ).astype(jnp.bfloat16)
    outgoing = outgoing.reshape(experts, slot_cap, model_dim)
    outgoing = jnp.broadcast_to(outgoing[:, None], (experts, x_count, slot_cap, model_dim))
    arrived = lax.all_to_all(
        outgoing.reshape(experts * x_count, slot_cap, model_dim), ("grp", "dev_0"), 0, 0, tiled=True
    )
    all_rows = lax.all_gather(arrived.reshape(-1, model_dim), "dev_1", axis=0, tiled=True)
    hid_units = gate_weight.shape[2]
    both_act = jnp.dot(
        all_rows,
        jnp.concatenate([gate_weight[0], up_weight[0]], axis=1),
        preferred_element_type=jnp.float32,
    )
    hidden = (jax.nn.silu(both_act[:, :hid_units]) * both_act[:, hid_units:]).astype(jnp.bfloat16)
    hidden = lax.optimization_barrier(hidden)
    partial_down = jnp.dot(hidden, down_weight[0], preferred_element_type=jnp.float32)
    summed = lax.psum_scatter(
        partial_down.astype(jnp.bfloat16), "dev_1", scatter_dimension=0, tiled=True
    )
    landed_back = lax.all_to_all(
        summed.reshape(experts * x_count, slot_cap, model_dim), ("grp", "dev_0"), 0, 0, tiled=True
    )
    returned = jnp.sum(
        landed_back.reshape(experts, x_count, slot_cap, model_dim).astype(jnp.float32), axis=1
    )
    weights = first_prob[:, None] * placed[:, 0, :] + second_prob[:, None] * placed[:, 1, :]
    contrib = jnp.dot(
        weights,
        returned.reshape(group_slots, model_dim),
        precision=HIGHEST_PREC,
    )
    return (hidden_float + contrib).astype(jnp.bfloat16)


def solution(mesh):
    torus = Mesh(mesh.devices.reshape(mesh.shape["grp"], 4, 8), ("grp", "dev_0", "dev_1"))
    in_specs = (
        P("grp", DEV),
        P("grp", DEV),
        P("grp", DEV),
        P(DEV),
        P("grp", None),
        P("grp", None),
        P(DEV),
        P(DEV),
        P(None, DEV),
        P(GRP_DEV, None),
        P(),
        P(),
        P(GRP_DEV, None),
        P("grp", None, DEV),
        P("grp", None, DEV),
        P("grp", DEV, None),
    )
    out_specs = P(GRP_DEV, None)
    return jax.shard_map(
        shards, mesh=torus, in_specs=in_specs, out_specs=out_specs, check_vma=False
    )
```

```python
import jax
import jax.numpy as jnp
from jax import lax
from jax.sharding import Mesh
from jax.sharding import PartitionSpec as P

GRP = ("grp_z", "grp_c")
DEV = ("dev_0", "dev_1")
GRP_DEV = (*GRP, "dev_0", "dev_1")


EPSILON = 1e-05
HIGHEST_PREC = lax.Precision.HIGHEST


def side_by_side(arrays, axis, dim, along):
    columns = [a.reshape(*a.shape[:along], -1) for a in arrays]
    both = jnp.concatenate(columns, axis=along)
    for part in axis[::-1]:
        both = lax.all_gather(both, part, axis=dim, tiled=True)
    filled, at, finished = (both, 0, [])
    for a, column in zip(arrays, columns):
        piece = filled[..., at : at + column.shape[along]]
        finished.append(piece.reshape(*piece.shape[:along], *a.shape[along:]))
        at += column.shape[along]
    return tuple(finished)


def sent_to_all(shard, axis):
    peers = lax.axis_size(axis)
    return lax.all_to_all(
        jnp.broadcast_to(shard[None], (peers, *shard.shape)), axis, 0, 0, tiled=True
    )


def of_everyone(shard, axis):
    everything = sent_to_all(shard, axis)
    return jnp.sum(everything, axis=0)


def in_order(tiles, dim):
    dims = list(tiles.shape[1:])
    dims[dim] *= tiles.shape[0]
    return jnp.moveaxis(tiles, 0, dim).reshape(dims)


def collect(shard, axis, dim):
    return in_order(sent_to_all(shard, axis), dim)


def sum_by_axis(terms, axes):
    total = terms.astype(jnp.bfloat16)
    for axis in axes:
        total = lax.psum_scatter(total, axis, scatter_dimension=0, tiled=True)
    return total.astype(jnp.float32)


def ring_gather(shard, axis):
    size = lax.axis_size(axis)
    forward, backward, pieces = shard, shard, {0: shard}
    for step in range(1, size // 2 + 1):
        forward = lax.ppermute(forward, axis, [(i, (i + 1) % size) for i in range(size)])
        pieces[-step] = forward
        if step < size - step:
            backward = lax.ppermute(backward, axis, [(i, (i - 1) % size) for i in range(size)])
            pieces[step] = backward
    offsets = list(range(-(size // 2), size - size // 2))
    stacked = jnp.stack([pieces[o] for o in offsets])
    doubled = jnp.concatenate([stacked, stacked])
    start = (-offsets[0] - lax.axis_index(axis)) % size
    return lax.dynamic_slice_in_dim(doubled, start, size, 0)


def rms_scale(values, gain_vec):
    return (
        values * lax.rsqrt(jnp.mean(values * values, axis=-1, keepdims=True) + EPSILON) * gain_vec
    )


def slot_tables(routes_block, expert_count, slot_cap):
    blocks, row_total = (routes_block.shape[0], routes_block.shape[1])
    flat_routes = routes_block.reshape(blocks, row_total * 2)
    onehot = (
        flat_routes[:, :, None] == jnp.arange(expert_count, dtype=jnp.int32)[None, None, :]
    ).astype(jnp.int32)
    earlier = jnp.cumsum(onehot, axis=1) - onehot
    slot_rank = jnp.sum(earlier * onehot, axis=2)
    slot_index = (flat_routes * slot_cap + slot_rank).reshape(blocks, row_total, 2)
    placed = (
        slot_index[:, :, :, None]
        == jnp.arange(expert_count * slot_cap, dtype=jnp.int32)[None, None, None, :]
    )
    return placed.astype(jnp.float32)


def shards(
    ssm_input,
    gate_input,
    step_size,
    decay_rate,
    in_coeff,
    out_coeff,
    skip_gain,
    norm_gain,
    out_proj,
    residual,
    ffn_gain,
    router,
    routes,
    gate_weight,
    up_weight,
    down_weight,
):
    tok_rows = ssm_input.shape[0]
    head_count = step_size.shape[1]
    head_width = ssm_input.shape[1] // head_count
    dev_count = lax.axis_size(DEV)
    inner_dim = ssm_input.shape[1] * dev_count
    block_rows = residual.shape[0]
    model_dim = residual.shape[1]
    experts = lax.axis_size(GRP)
    slot_cap = max(2, 4 * block_rows // experts)
    group_slots = experts * slot_cap
    inputs_f = ssm_input.astype(jnp.float32).reshape(tok_rows, head_count, head_width)
    in_float = in_coeff.astype(jnp.float32)
    out_float = out_coeff.astype(jnp.float32)
    log_rate = -(step_size * decay_rate[None, :])
    cumulative = jnp.cumsum(log_rate, axis=0)
    causal = (jnp.arange(tok_rows)[:, None] >= jnp.arange(tok_rows)[None, :])[:, :, None]
    spread = cumulative[:, None, :] - cumulative[None, :, :]
    decay_pair = jnp.where(causal, jnp.exp(jnp.where(causal, spread, 0.0)), 0.0)
    scores = jnp.dot(out_coeff, in_coeff.T, preferred_element_type=jnp.float32)
    mixing = decay_pair * scores[:, :, None] * step_size[None, :, :]
    inside = jnp.einsum("tuh,uhp->thp", mixing, inputs_f, precision=HIGHEST_PREC)
    to_end = jnp.exp(cumulative[-1][None, :] - cumulative) * step_size
    own_state = jnp.einsum("uh,uhp,un->hpn", to_end, inputs_f, in_float, precision=HIGHEST_PREC)
    own_log = cumulative[-1]
    group_logs, group_states = tuple(
        (
            part.astype(jnp.float32)
            for part in side_by_side(
                (own_log[None].astype(jnp.bfloat16), own_state[None].astype(jnp.bfloat16)),
                GRP,
                0,
                2,
            )
        )
    )
    group_index = jnp.arange(group_logs.shape[0])
    my_group = lax.axis_index(GRP)
    inclusive = jnp.cumsum(group_logs, axis=0)
    exclusive = inclusive - group_logs
    before_me = jnp.sum(jnp.where((group_index == my_group)[:, None], exclusive, 0.0), axis=0)
    earlier_mask = (group_index < my_group)[:, None]
    weighting = jnp.where(
        earlier_mask, jnp.exp(jnp.where(earlier_mask, before_me[None, :] - inclusive, 0.0)), 0.0
    )
    entering = jnp.einsum("gh,ghpn->hpn", weighting, group_states, precision=HIGHEST_PREC)
    carried = jnp.exp(cumulative)[:, :, None] * jnp.einsum(
        "hpn,tn->thp", entering, out_float, precision=HIGHEST_PREC
    )
    ssm_out = inside + carried + skip_gain[None, :, None] * inputs_f
    gated_out = ssm_out.reshape(tok_rows, head_count * head_width) * jax.nn.silu(
        gate_input.astype(jnp.float32)
    )
    gated_gain = gated_out * norm_gain[None, :]
    squares = gated_out * gated_out
    proj_rows = lax.all_to_all(
        out_proj.reshape(dev_count, -1, out_proj.shape[1]), DEV, 0, 0, tiled=True
    )
    chan = proj_rows.shape[1]
    proj_rows = jnp.transpose(proj_rows, (1, 0, 2)).reshape(chan, model_dim)
    lane_pad = 128
    square_cols = (jnp.arange(lane_pad) == 0).astype(jnp.bfloat16)
    rhs = jnp.concatenate(
        [
            jnp.concatenate([proj_rows, jnp.zeros((chan, lane_pad), jnp.bfloat16)], axis=1),
            jnp.concatenate(
                [jnp.zeros((chan, model_dim), jnp.bfloat16), jnp.broadcast_to(square_cols, (chan, lane_pad))],
                axis=1,
            ),
        ],
        axis=0,
    )
    lhs = jnp.concatenate([gated_gain, squares], axis=1).astype(jnp.bfloat16)
    payload = jnp.dot(lhs, rhs, preferred_element_type=jnp.float32).astype(jnp.bfloat16)
    x_count = lax.axis_size("dev_0")
    y_count = lax.axis_size("dev_1")
    by_x = lax.all_to_all(
        payload.reshape(x_count, y_count, block_rows, payload.shape[1]), "dev_0", 0, 0, tiled=True
    )
    by_x = jnp.sum(by_x.astype(jnp.float32), axis=0).astype(jnp.bfloat16)
    landed = lax.all_to_all(by_x, "dev_1", 0, 0, tiled=True)
    landed = jnp.sum(landed.astype(jnp.float32), axis=0)
    summed_proj = landed[:, :model_dim]
    token_squares = landed[:, model_dim]
    mamba_out = (
        summed_proj * lax.rsqrt(token_squares / inner_dim + EPSILON)[:, None]
    ).astype(jnp.bfloat16)
    hidden_res = (residual.astype(jnp.float32) + mamba_out.astype(jnp.float32)).astype(jnp.bfloat16)
    hidden_float = hidden_res.astype(jnp.float32)
    normed = rms_scale(hidden_float, ffn_gain).astype(jnp.bfloat16)
    logits = jnp.dot(normed.astype(jnp.float32), router, precision=HIGHEST_PREC)
    expert_ids = jnp.arange(experts, dtype=jnp.int32)[None, :]
    first_logit = jnp.sum(logits * (routes[:, 0:1] == expert_ids).astype(jnp.float32), axis=1)
    second_logit = jnp.sum(logits * (routes[:, 1:2] == expert_ids).astype(jnp.float32), axis=1)
    first_prob = jax.nn.sigmoid(first_logit - second_logit)
    second_prob = 1.0 - first_prob
    placed = slot_tables(routes[None], experts, slot_cap)[0]
    filled = jnp.sum(placed, axis=1)
    outgoing = jnp.dot(
        filled.T.astype(jnp.bfloat16), normed, preferred_element_type=jnp.float32
    ).astype(jnp.bfloat16)
    outgoing = outgoing.reshape(experts, slot_cap, model_dim)
    outgoing = jnp.broadcast_to(outgoing[:, None], (experts, x_count, slot_cap, model_dim))
    arrived = lax.all_to_all(
        outgoing.reshape(experts * x_count, slot_cap, model_dim), (*GRP, "dev_0"), 0, 0, tiled=True
    )
    all_rows = lax.all_gather(arrived.reshape(-1, model_dim), "dev_1", axis=0, tiled=True)
    hid_units = gate_weight.shape[2]
    both_act = jnp.dot(
        all_rows,
        jnp.concatenate([gate_weight[0], up_weight[0]], axis=1),
        preferred_element_type=jnp.float32,
    )
    hidden = (jax.nn.silu(both_act[:, :hid_units]) * both_act[:, hid_units:]).astype(jnp.bfloat16)
    hidden = lax.optimization_barrier(hidden)
    partial_down = jnp.dot(hidden, down_weight[0], preferred_element_type=jnp.float32)
    summed = lax.psum_scatter(
        partial_down.astype(jnp.bfloat16), "dev_1", scatter_dimension=0, tiled=True
    )
    landed_back = lax.all_to_all(
        summed.reshape(experts * x_count, slot_cap, model_dim), (*GRP, "dev_0"), 0, 0, tiled=True
    )
    returned = jnp.sum(
        landed_back.reshape(experts, x_count, slot_cap, model_dim).astype(jnp.float32), axis=1
    )
    weights = first_prob[:, None] * placed[:, 0, :] + second_prob[:, None] * placed[:, 1, :]
    contrib = jnp.dot(
        weights,
        returned.reshape(group_slots, model_dim),
        precision=HIGHEST_PREC,
    )
    return (hidden_float + contrib).astype(jnp.bfloat16)


def solution(mesh):
    torus = Mesh(mesh.devices.reshape(mesh.shape["grp"] // 2, 2, 4, 8), (*GRP, "dev_0", "dev_1"))
    in_specs = (
        P(GRP, DEV),
        P(GRP, DEV),
        P(GRP, DEV),
        P(DEV),
        P(GRP, None),
        P(GRP, None),
        P(DEV),
        P(DEV),
        P(None, DEV),
        P(GRP_DEV, None),
        P(),
        P(),
        P(GRP_DEV, None),
        P(GRP, None, DEV),
        P(GRP, None, DEV),
        P(GRP, DEV, None),
    )
    out_specs = P(GRP_DEV, None)
    return jax.shard_map(
        shards, mesh=torus, in_specs=in_specs, out_specs=out_specs, check_vma=False
    )
```

```python
import jax
import jax.numpy as jnp
from jax import lax
from jax.sharding import Mesh
from jax.sharding import PartitionSpec as P

DEV = ("dev_0", "dev_1")
GRP_DEV = ("grp", "dev_0", "dev_1")


EPSILON = 1e-05
HIGHEST_PREC = lax.Precision.HIGHEST


def side_by_side(arrays, axis, dim, along):
    columns = [a.reshape(*a.shape[:along], -1) for a in arrays]
    both = jnp.concatenate(columns, axis=along)
    filled, at, finished = (lax.all_gather(both, axis, axis=dim, tiled=True), 0, [])
    for a, column in zip(arrays, columns):
        piece = filled[..., at : at + column.shape[along]]
        finished.append(piece.reshape(*piece.shape[:along], *a.shape[along:]))
        at += column.shape[along]
    return tuple(finished)


def sent_to_all(shard, axis):
    peers = lax.axis_size(axis)
    return lax.all_to_all(
        jnp.broadcast_to(shard[None], (peers, *shard.shape)), axis, 0, 0, tiled=True
    )


def of_everyone(shard, axis):
    everything = sent_to_all(shard, axis)
    return jnp.sum(everything, axis=0)


def in_order(tiles, dim):
    dims = list(tiles.shape[1:])
    dims[dim] *= tiles.shape[0]
    return jnp.moveaxis(tiles, 0, dim).reshape(dims)


def collect(shard, axis, dim):
    return in_order(sent_to_all(shard, axis), dim)


def sum_by_axis(terms, axes):
    total = terms.astype(jnp.bfloat16)
    for axis in axes:
        total = lax.psum_scatter(total, axis, scatter_dimension=0, tiled=True)
    return total.astype(jnp.float32)


def ring_gather(shard, axis):
    size = lax.axis_size(axis)
    forward, backward, pieces = shard, shard, {0: shard}
    for step in range(1, size // 2 + 1):
        forward = lax.ppermute(forward, axis, [(i, (i + 1) % size) for i in range(size)])
        pieces[-step] = forward
        if step < size - step:
            backward = lax.ppermute(backward, axis, [(i, (i - 1) % size) for i in range(size)])
            pieces[step] = backward
    offsets = list(range(-(size // 2), size - size // 2))
    stacked = jnp.stack([pieces[o] for o in offsets])
    doubled = jnp.concatenate([stacked, stacked])
    start = (-offsets[0] - lax.axis_index(axis)) % size
    return lax.dynamic_slice_in_dim(doubled, start, size, 0)


def rms_scale(values, gain_vec):
    return (
        values * lax.rsqrt(jnp.mean(values * values, axis=-1, keepdims=True) + EPSILON) * gain_vec
    )


def slot_tables(routes_block, expert_count, slot_cap):
    blocks, row_total = (routes_block.shape[0], routes_block.shape[1])
    flat_routes = routes_block.reshape(blocks, row_total * 2)
    onehot = (
        flat_routes[:, :, None] == jnp.arange(expert_count, dtype=jnp.int32)[None, None, :]
    ).astype(jnp.int32)
    earlier = jnp.cumsum(onehot, axis=1) - onehot
    slot_rank = jnp.sum(earlier * onehot, axis=2)
    slot_index = (flat_routes * slot_cap + slot_rank).reshape(blocks, row_total, 2)
    placed = (
        slot_index[:, :, :, None]
        == jnp.arange(expert_count * slot_cap, dtype=jnp.int32)[None, None, None, :]
    )
    return placed.astype(jnp.float32)


def shards(
    ssm_input,
    gate_input,
    step_size,
    decay_rate,
    in_coeff,
    out_coeff,
    skip_gain,
    norm_gain,
    out_proj,
    residual,
    ffn_gain,
    router,
    routes,
    gate_weight,
    up_weight,
    down_weight,
):
    tok_rows = ssm_input.shape[0]
    head_count = step_size.shape[1]
    head_width = ssm_input.shape[1] // head_count
    dev_count = lax.axis_size(DEV)
    inner_dim = ssm_input.shape[1] * dev_count
    block_rows = residual.shape[0]
    model_dim = residual.shape[1]
    experts = lax.axis_size("grp")
    slot_cap = max(2, 4 * block_rows // experts)
    group_slots = experts * slot_cap
    inputs_f = ssm_input.astype(jnp.float32).reshape(tok_rows, head_count, head_width)
    in_float = in_coeff.astype(jnp.float32)
    out_float = out_coeff.astype(jnp.float32)
    log_rate = -(step_size * decay_rate[None, :])
    cumulative = jnp.cumsum(log_rate, axis=0)
    causal = (jnp.arange(tok_rows)[:, None] >= jnp.arange(tok_rows)[None, :])[:, :, None]
    spread = cumulative[:, None, :] - cumulative[None, :, :]
    decay_pair = jnp.where(causal, jnp.exp(jnp.where(causal, spread, 0.0)), 0.0)
    scores = jnp.dot(out_coeff, in_coeff.T, preferred_element_type=jnp.float32)
    mixing = decay_pair * scores[:, :, None] * step_size[None, :, :]
    inside = jnp.einsum("tuh,uhp->thp", mixing, inputs_f, precision=HIGHEST_PREC)
    to_end = jnp.exp(cumulative[-1][None, :] - cumulative) * step_size
    own_state = jnp.einsum("uh,uhp,un->hpn", to_end, inputs_f, in_float, precision=HIGHEST_PREC)
    own_log = cumulative[-1]
    group_logs, group_states = tuple(
        (
            part.astype(jnp.float32)
            for part in side_by_side(
                (own_log[None].astype(jnp.bfloat16), own_state[None].astype(jnp.bfloat16)),
                "grp",
                0,
                2,
            )
        )
    )
    group_index = jnp.arange(group_logs.shape[0])
    my_group = lax.axis_index("grp")
    inclusive = jnp.cumsum(group_logs, axis=0)
    exclusive = inclusive - group_logs
    before_me = jnp.sum(jnp.where((group_index == my_group)[:, None], exclusive, 0.0), axis=0)
    earlier_mask = (group_index < my_group)[:, None]
    weighting = jnp.where(
        earlier_mask, jnp.exp(jnp.where(earlier_mask, before_me[None, :] - inclusive, 0.0)), 0.0
    )
    entering = jnp.einsum("gh,ghpn->hpn", weighting, group_states, precision=HIGHEST_PREC)
    carried = jnp.exp(cumulative)[:, :, None] * jnp.einsum(
        "hpn,tn->thp", entering, out_float, precision=HIGHEST_PREC
    )
    ssm_out = inside + carried + skip_gain[None, :, None] * inputs_f
    gated_out = ssm_out.reshape(tok_rows, head_count * head_width) * jax.nn.silu(
        gate_input.astype(jnp.float32)
    )
    gated_gain = gated_out * norm_gain[None, :]
    squares = gated_out * gated_out
    proj_rows = lax.all_to_all(
        out_proj.reshape(dev_count, -1, out_proj.shape[1]), DEV, 0, 0, tiled=True
    )
    chan = proj_rows.shape[1]
    proj_rows = jnp.transpose(proj_rows, (1, 0, 2)).reshape(chan, model_dim)
    lane_pad = 128
    square_cols = (jnp.arange(lane_pad) == 0).astype(jnp.bfloat16)
    rhs = jnp.concatenate(
        [
            jnp.concatenate([proj_rows, jnp.zeros((chan, lane_pad), jnp.bfloat16)], axis=1),
            jnp.concatenate(
                [jnp.zeros((chan, model_dim), jnp.bfloat16), jnp.broadcast_to(square_cols, (chan, lane_pad))],
                axis=1,
            ),
        ],
        axis=0,
    )
    lhs = jnp.concatenate([gated_gain, squares], axis=1).astype(jnp.bfloat16)
    payload = jnp.dot(lhs, rhs, preferred_element_type=jnp.float32).astype(jnp.bfloat16)
    x_count = lax.axis_size("dev_0")
    y_count = lax.axis_size("dev_1")
    by_x = lax.all_to_all(
        payload.reshape(x_count, y_count, block_rows, payload.shape[1]), "dev_0", 0, 0, tiled=True
    )
    both_weight = jnp.concatenate([gate_weight[0], up_weight[0]], axis=1)
    by_x, both_weight = lax.optimization_barrier((by_x, both_weight))
    by_x = jnp.sum(by_x.astype(jnp.float32), axis=0).astype(jnp.bfloat16)
    landed = lax.all_to_all(by_x, "dev_1", 0, 0, tiled=True)
    landed = jnp.sum(landed.astype(jnp.float32), axis=0)
    summed_proj = landed[:, :model_dim]
    token_squares = landed[:, model_dim]
    mamba_out = (
        summed_proj * lax.rsqrt(token_squares / inner_dim + EPSILON)[:, None]
    ).astype(jnp.bfloat16)
    hidden_res = (residual.astype(jnp.float32) + mamba_out.astype(jnp.float32)).astype(jnp.bfloat16)
    hidden_float = hidden_res.astype(jnp.float32)
    normed = rms_scale(hidden_float, ffn_gain).astype(jnp.bfloat16)
    logits = jnp.dot(normed.astype(jnp.float32), router, precision=HIGHEST_PREC)
    expert_ids = jnp.arange(experts, dtype=jnp.int32)[None, :]
    first_logit = jnp.sum(logits * (routes[:, 0:1] == expert_ids).astype(jnp.float32), axis=1)
    second_logit = jnp.sum(logits * (routes[:, 1:2] == expert_ids).astype(jnp.float32), axis=1)
    first_prob = jax.nn.sigmoid(first_logit - second_logit)
    second_prob = 1.0 - first_prob
    placed = slot_tables(routes[None], experts, slot_cap)[0]
    filled = jnp.sum(placed, axis=1)
    outgoing = jnp.dot(
        filled.T.astype(jnp.bfloat16), normed, preferred_element_type=jnp.float32
    ).astype(jnp.bfloat16)
    outgoing = outgoing.reshape(experts, slot_cap, model_dim)
    outgoing = jnp.broadcast_to(outgoing[:, None], (experts, x_count, slot_cap, model_dim))
    arrived = lax.all_to_all(
        outgoing.reshape(experts * x_count, slot_cap, model_dim), ("grp", "dev_0"), 0, 0, tiled=True
    )
    all_rows = lax.all_gather(arrived.reshape(-1, model_dim), "dev_1", axis=0, tiled=True)
    hid_units = gate_weight.shape[2]
    both_act = jnp.dot(
        all_rows,
        both_weight,
        preferred_element_type=jnp.float32,
    )
    hidden = (jax.nn.silu(both_act[:, :hid_units]) * both_act[:, hid_units:]).astype(jnp.bfloat16)
    hidden = lax.optimization_barrier(hidden)
    partial_down = jnp.dot(hidden, down_weight[0], preferred_element_type=jnp.float32)
    summed = lax.psum_scatter(
        partial_down.astype(jnp.bfloat16), "dev_1", scatter_dimension=0, tiled=True
    )
    landed_back = lax.all_to_all(
        summed.reshape(experts * x_count, slot_cap, model_dim), ("grp", "dev_0"), 0, 0, tiled=True
    )
    returned = jnp.sum(
        landed_back.reshape(experts, x_count, slot_cap, model_dim).astype(jnp.float32), axis=1
    )
    weights = first_prob[:, None] * placed[:, 0, :] + second_prob[:, None] * placed[:, 1, :]
    contrib = jnp.dot(
        weights,
        returned.reshape(group_slots, model_dim),
        precision=HIGHEST_PREC,
    )
    return (hidden_float + contrib).astype(jnp.bfloat16)


def solution(mesh):
    torus = Mesh(mesh.devices.reshape(mesh.shape["grp"], 4, 8), ("grp", "dev_0", "dev_1"))
    in_specs = (
        P("grp", DEV),
        P("grp", DEV),
        P("grp", DEV),
        P(DEV),
        P("grp", None),
        P("grp", None),
        P(DEV),
        P(DEV),
        P(None, DEV),
        P(GRP_DEV, None),
        P(),
        P(),
        P(GRP_DEV, None),
        P("grp", None, DEV),
        P("grp", None, DEV),
        P("grp", DEV, None),
    )
    out_specs = P(GRP_DEV, None)
    return jax.shard_map(
        shards, mesh=torus, in_specs=in_specs, out_specs=out_specs, check_vma=False
    )
```
